256 devices in a mesh: ctx: 32 (over y, x, core), head: 8 (over z).
Axes of the slice: x: 4, y: 4, z: 8, core: 2. Of those that a mesh axis runs over, the one named last changes fastest.
Arguments:
- ssm_input: bfloat16 [8192, 8192], P('ctx', 'head'), may hold values from -6 to 6
- gate_input: bfloat16 [8192, 8192], P('ctx', 'head'), may hold values from -6 to 6
- step_raw: float32 [8192, 128], P('ctx', 'head'), may hold values from -4 to 4
- b_matrix: bfloat16 [8192, 1024], P('ctx', 'head'), may hold values from -6 to 6
- c_matrix: bfloat16 [8192, 1024], P('ctx', 'head'), may hold values from -6 to 6
- step_bias: float32 [128], P('head'), may hold values from -6 to -4
- log_rate: float32 [128], P('head')
- skip_gain: float32 [128], P('head'), may hold values from 0.5 to 1.5
- norm_weight: float32 [8192], P('head'), may hold values from 0.5 to 1.5
- doc_resets: int32 [8192], P('ctx'), may hold values from 0 to 1, as said below
- grad_output: bfloat16 [8192, 8192], P('ctx', 'head'), may hold values from -6 to 6
Outputs:
- grad_input: bfloat16 [8192, 8192], P('ctx', 'head')
- grad_gate: bfloat16 [8192, 8192], P('ctx', 'head')
- grad_step: float32 [8192, 128], P('ctx', 'head')
- grad_b_matrix: float32 [8192, 1024], P('ctx', 'head')
- grad_c_matrix: float32 [8192, 1024], P('ctx', 'head')
The draws below stay inside these ranges and needn't reach their ends.
Inputs may be any that keep to these rules, and one draw needn't show every extreme that they name: `doc_resets`: exactly 4 positions hold 1, all of them among positions 1 to 127; all others hold 0.
All inputs are finite; a program needn't handle non-finite values.
Results may differ from the reference program's by a relative error of at most 0.001.
Values sent between devices are 32-bit elements; how exact they have to be, the bound alone decides.
No kernel may reach another device: no remote copies, remote signals or barrier semaphores. Data moves between devices by JAX's collectives and lax.ppermute only.
A program may use at most 64 MiB of HBM per device.

```python
import jax
import jax.numpy as jnp
from jax import lax

HEADS = 128
HEAD_DIM = 64
STATE = 128
GROUPS = 8
SPAN = 256
DOCS = 4
TOK_DEV = 256
TOKENS = 8192
D_INNER = 8192


def draw_log_rate(key, part):
    key_pick, key_slow, key_fast = jax.random.split(key, 3)
    share = 0.5
    picked = jax.random.uniform(key_pick, (HEADS,), jnp.float32)
    slow_rate = jnp.log(20.0 / TOKENS) + jax.random.uniform(key_slow, (HEADS,), jnp.float32) * jnp.log(10.0)
    fast_rate = jax.random.uniform(key_fast, (HEADS,), jnp.float32) * jnp.log(8.0)
    return jnp.where(picked < share, slow_rate, fast_rate)


def draw_doc_resets(key, part):
    starts = jax.random.permutation(key, TOK_DEV // 2 - 1)[:DOCS] + 1
    return jnp.zeros((TOKENS,), jnp.int32).at[starts].set(1)


def steps_of(key, dims, cuts, low, largest):
    gain, own = 1.0, jax.random.fold_in(key, 6)
    for axis_at, blocks in cuts:
        steps = jnp.exp(jax.random.uniform(jax.random.fold_in(own, axis_at), (blocks,), jnp.float32, low / len(cuts), largest / len(cuts)))
        gain = gain * jnp.repeat(steps, dims[axis_at] // blocks).reshape([-1 if axis == axis_at else 1 for axis in range(len(dims))])
    return gain


def gaussian(rng, extent, deviation, limit, cuts=(), kind=jnp.bfloat16):
    array = deviation * jax.random.normal(rng, extent, jnp.float32)
    if cuts:
        array = array * steps_of(rng, extent, cuts, -0.22, 0.18)
    return jnp.clip(array, -limit, limit).astype(kind)


def setup_inputs(seed: int = 0) -> dict:
    arg_keys = jax.random.split(jax.random.key(seed), 12)
    ssm_input = gaussian(arg_keys[0], (TOKENS, D_INNER), 1.0, 6.0, ((0, 32), (1, 8)))
    gate_input = gaussian(arg_keys[1], (TOKENS, D_INNER), 1.0, 6.0, ((0, 32), (1, 8)))
    step_raw = gaussian(arg_keys[2], (TOKENS, HEADS), 1.0, 4.0, ((0, 32), (1, 8)), jnp.float32)
    b_matrix = gaussian(arg_keys[3], (TOKENS, GROUPS * STATE), 1.0, 6.0, ((0, 32), (1, 8)))
    c_matrix = gaussian(arg_keys[4], (TOKENS, GROUPS * STATE), 1.0, 6.0, ((0, 32), (1, 8)))
    step_bias = jnp.clip(-6.0 + 2.0 * jax.random.uniform(arg_keys[5], (HEADS,), jnp.float32) ** steps_of(arg_keys[5], (HEADS,), ((0, 8),), -0.2, 0.2), -6.0, -4.0)
    log_rate = draw_log_rate(jax.random.fold_in(arg_keys[11], 71), 0)
    skip_gain = jnp.clip(0.5 + 1.0 * jax.random.uniform(arg_keys[7], (HEADS,), jnp.float32) ** steps_of(arg_keys[7], (HEADS,), ((0, 8),), -0.2, 0.2), 0.5, 1.5)
    norm_weight = jnp.clip(0.5 + 1.0 * jax.random.uniform(arg_keys[8], (D_INNER,), jnp.float32) ** steps_of(arg_keys[8], (D_INNER,), ((0, 8),), -0.2, 0.2), 0.5, 1.5)
    doc_resets = draw_doc_resets(jax.random.fold_in(arg_keys[11], 71), 0)
    grad_output = gaussian(arg_keys[10], (TOKENS, D_INNER), 1.0, 6.0, ((0, 32), (1, 8)))
    return dict(ssm_input=ssm_input, gate_input=gate_input, step_raw=step_raw, b_matrix=b_matrix, c_matrix=c_matrix, step_bias=step_bias, log_rate=log_rate, skip_gain=skip_gain, norm_weight=norm_weight, doc_resets=doc_resets, grad_output=grad_output)


HIGHEST_PRECISION = lax.Precision.HIGHEST
EPSILON = 1e-05

def span_mix(x_span, dt_span, b_span, c_span, log_cum, segment):
    log_rows = jnp.moveaxis(log_cum, 0, -1)
    spread = log_rows[..., :, None] - log_rows[..., None, :]
    places = jnp.arange(x_span.shape[0], dtype=jnp.int32)
    keep_mask = ((places[:, None] >= places[None, :]) & (segment[:, None] == segment[None, :])).astype(jnp.float32)
    masked = jnp.exp(jnp.minimum(spread, 0.0)) * keep_mask
    scores = jnp.einsum('tgn,sgn->gts', c_span, b_span, precision=HIGHEST_PRECISION)
    weights = scores[:, None] * masked * jnp.moveaxis(dt_span, 0, -1)[..., None, :]
    return jnp.einsum('ghts,sghp->tghp', weights, x_span, precision=HIGHEST_PRECISION)

def layer_output(ssm_input, gate_input, step_raw, b_matrix, c_matrix, step_bias, log_rate, skip_gain, norm_weight, doc_resets):
    per_group = HEADS // GROUPS
    spans = TOKENS // SPAN
    step_size = jax.nn.softplus(step_raw + step_bias[None, :])
    decay_rate = (-jnp.exp(log_rate)).reshape(GROUPS, per_group)
    x_spans = ssm_input.reshape(spans, SPAN, GROUPS, per_group, HEAD_DIM)
    dt_spans = step_size.reshape(spans, SPAN, GROUPS, per_group)
    b_spans = b_matrix.reshape(spans, SPAN, GROUPS, STATE)
    c_spans = c_matrix.reshape(spans, SPAN, GROUPS, STATE)
    reset_spans = doc_resets.reshape(spans, SPAN)

    def advance(carry_state, pieces):
        x_span, dt_span, b_span, c_span, reset_span = pieces
        log_cum = jnp.cumsum(dt_span * decay_rate, axis=0)
        segment = jnp.cumsum(reset_span, dtype=jnp.int32)
        inner_part = span_mix(x_span, dt_span, b_span, c_span, log_cum, segment)
        opened = (segment == 0).astype(jnp.float32)
        entry_decay = jnp.exp(log_cum) * opened[:, None, None]
        carried = jnp.einsum('tgn,ghpn->tghp', c_span, carry_state, precision=HIGHEST_PRECISION) * entry_decay[..., None]
        closing = segment[-1]
        tail_decay = jnp.exp(log_cum[-1] - log_cum) * (segment == closing).astype(jnp.float32)[:, None, None]
        added_terms = jnp.einsum('sgh,sghp,sgn->ghpn', tail_decay * dt_span, x_span, b_span, precision=HIGHEST_PRECISION)
        through = jnp.exp(log_cum[-1]) * (closing == 0).astype(jnp.float32)
        return (through[..., None, None] * carry_state + added_terms, inner_part + carried)
    zero_state = jnp.zeros((GROUPS, per_group, HEAD_DIM, STATE), jnp.float32)
    _, mixed = lax.scan(jax.checkpoint(advance), zero_state, (x_spans, dt_spans, b_spans, c_spans, reset_spans))
    core_out = mixed.reshape(TOKENS, HEADS * HEAD_DIM) + ssm_input * jnp.repeat(skip_gain, HEAD_DIM)[None, :]
    gated = core_out * jax.nn.silu(gate_input)
    inv_rms = lax.rsqrt(lax.optimization_barrier(jnp.mean(gated * gated, axis=1, keepdims=True)) + EPSILON)
    return gated * inv_rms * norm_weight[None, :]

def reference(ssm_input, gate_input, step_raw, b_matrix, c_matrix, step_bias, log_rate, skip_gain, norm_weight, doc_resets, grad_output):

    def loss_map(x_value, gate_value, step_value, b_value, c_value):
        return layer_output(x_value, gate_value, step_value, b_value, c_value, step_bias, log_rate, skip_gain, norm_weight, doc_resets)
    _, backward = jax.vjp(loss_map, ssm_input.astype(jnp.float32), gate_input.astype(jnp.float32), step_raw, b_matrix.astype(jnp.float32), c_matrix.astype(jnp.float32))
    grad_x, grad_g, grad_s, grad_b, grad_c = backward(grad_output.astype(jnp.float32))
    return (grad_x.astype(jnp.bfloat16), grad_g.astype(jnp.bfloat16), grad_s, grad_b, grad_c)
```

```python
import jax
import jax.numpy as jnp
from jax import lax
from jax.sharding import PartitionSpec as P

HEAD_DIM = 64
STATE = 128
SPAN = 256


HIGHEST_PRECISION = lax.Precision.HIGHEST
EPSILON = 1e-05


def exclusive_scan(gain, value, axis, forward):
    size = lax.axis_size(axis)
    total = jnp.zeros_like(value)
    total_gain = jnp.ones_like(gain)
    distance = 1
    while distance < size:
        if forward:
            pairs = [(i, i + distance) for i in range(size - distance)]
        else:
            pairs = [(i + distance, i) for i in range(size - distance)]
        gain_in, value_in = lax.ppermute((gain, value), axis, pairs)
        total = total + total_gain[..., None, None] * value_in
        distance *= 2
        if distance < size:
            total_gain = total_gain * gain_in
            value = value + gain[..., None, None] * value_in
            gain = gain * gain_in
    return total


def span_mix(x_span, dt_span, b_span, c_span, log_cum, segment):
    log_rows = jnp.moveaxis(log_cum, 0, -1)
    spread = log_rows[..., :, None] - log_rows[..., None, :]
    places = jnp.arange(x_span.shape[0], dtype=jnp.int32)
    keep_mask = (
        (places[:, None] >= places[None, :]) & (segment[:, None] == segment[None, :])
    ).astype(jnp.float32)
    masked = jnp.exp(jnp.minimum(spread, 0.0)) * keep_mask
    scores = jnp.einsum("tgn,sgn->gts", c_span, b_span, precision=HIGHEST_PRECISION)
    weights = scores[:, None] * masked * jnp.moveaxis(dt_span, 0, -1)[..., None, :]
    return jnp.einsum("ghts,sghp->tghp", weights, x_span, precision=HIGHEST_PRECISION)


def block_decays(dt_spans, segment, decay_rate):
    log_cum = jnp.cumsum(dt_spans * decay_rate, axis=1)
    closing = segment[:, -1]
    through = jnp.exp(log_cum[:, -1]) * (closing == 0).astype(jnp.float32)[:, None, None]
    return (log_cum, closing, through)


def local_states(x_spans, dt_spans, b_spans, segment, decay_rate):
    log_cum, closing, through = block_decays(dt_spans, segment, decay_rate)
    same_doc = (segment == closing[:, None]).astype(jnp.float32)
    tail_decay = jnp.exp(log_cum[:, -1:] - log_cum) * same_doc[:, :, None, None]
    added_terms = jnp.einsum(
        "kqgh,kqghp,kqgn->kghpn",
        tail_decay * dt_spans,
        x_spans,
        b_spans,
        precision=HIGHEST_PRECISION,
    )

    def advance(carried_pair, item_pair):
        carry_state, product = carried_pair
        decay_now, fresh_state = item_pair
        return (
            (decay_now[..., None, None] * carry_state + fresh_state, product * decay_now),
            carry_state,
        )

    initial = (
        jnp.zeros(added_terms.shape[1:], jnp.float32),
        jnp.ones(through.shape[1:], jnp.float32),
    )
    (final_state, product), starts = lax.scan(advance, initial, (through, added_terms))
    return (starts, final_state, product)


def output_part(x_spans, dt_spans, b_spans, c_spans, segment, decay_rate, starts, entry_state):
    log_cum, closing, through = block_decays(dt_spans, segment, decay_rate)

    def rolling(product, decay_now):
        return (product * decay_now, product)

    _, before = lax.scan(rolling, jnp.ones(through.shape[1:], jnp.float32), through)
    full_start = starts + before[..., None, None] * entry_state[None]
    opened = (segment == 0).astype(jnp.float32)
    entry_decay = jnp.exp(log_cum) * opened[:, :, None, None]
    carried = (
        jnp.einsum("kqgn,kghpn->kqghp", c_spans, full_start, precision=HIGHEST_PRECISION)
        * entry_decay[..., None]
    )
    mix_block = jax.checkpoint(lambda pieces: span_mix(*pieces))
    inner_part = lax.map(mix_block, (x_spans, dt_spans, b_spans, c_spans, log_cum, segment))
    return inner_part + carried


def body(
    ssm_input,
    gate_input,
    step_raw,
    b_matrix,
    c_matrix,
    step_bias,
    log_rate,
    skip_gain,
    norm_weight,
    doc_resets,
    grad_output,
):
    tokens_here = ssm_input.shape[0]
    heads_here = step_raw.shape[1]
    groups_here = b_matrix.shape[1] // STATE
    per_group = heads_here // groups_here
    spans = tokens_here // SPAN
    x_float = ssm_input.astype(jnp.float32)
    gate_float = gate_input.astype(jnp.float32)
    shifted = step_raw + step_bias[None, :]
    step_size = jax.nn.softplus(shifted)
    decay_rate = (-jnp.exp(log_rate)).reshape(groups_here, per_group)
    x_spans = x_float.reshape(spans, SPAN, groups_here, per_group, HEAD_DIM)
    dt_spans = step_size.reshape(spans, SPAN, groups_here, per_group)
    b_spans = b_matrix.astype(jnp.float32).reshape(spans, SPAN, groups_here, STATE)
    c_spans = c_matrix.astype(jnp.float32).reshape(spans, SPAN, groups_here, STATE)
    segment = jnp.cumsum(doc_resets.reshape(spans, SPAN), axis=1, dtype=jnp.int32)

    def states_call(x_value, dt_value, b_value):
        return local_states(x_value, dt_value, b_value, segment, decay_rate)

    (starts, end_local, through_all), states_back = jax.vjp(states_call, x_spans, dt_spans, b_spans)
    entry_state = exclusive_scan(through_all, end_local, "ctx", True)

    def output_call(x_value, dt_value, b_value, c_value, start_value, entry_value):
        return output_part(
            x_value, dt_value, b_value, c_value, segment, decay_rate, start_value, entry_value
        )

    core_part, output_back = jax.vjp(
        output_call, x_spans, dt_spans, b_spans, c_spans, starts, entry_state
    )
    skip_cols = jnp.repeat(skip_gain, HEAD_DIM)[None, :]
    core_out = core_part.reshape(tokens_here, heads_here * HEAD_DIM) + x_float * skip_cols
    gate_sig = jax.nn.sigmoid(gate_float)
    gate_act = gate_float * gate_sig
    gated = core_out * gate_act
    weighted_grad = norm_weight[None, :] * grad_output.astype(jnp.float32)
    norm_width = lax.axis_size("head") * gated.shape[1]
    sums = lax.psum(
        jnp.stack([jnp.sum(gated * gated, axis=1), jnp.sum(weighted_grad * gated, axis=1)]),
        "head",
    )
    inv_rms = lax.rsqrt(sums[0] / norm_width + EPSILON)
    normed = gated * inv_rms[:, None]
    product = sums[1] * inv_rms
    grad_gated = inv_rms[:, None] * (weighted_grad - normed * (product / norm_width)[:, None])
    grad_core = grad_gated * gate_act
    grad_gate = grad_gated * core_out * gate_sig * (1.0 + gate_float * (1.0 - gate_sig))
    first_grads = output_back(grad_core.reshape(core_part.shape))
    exit_adjoint = exclusive_scan(through_all, first_grads[5], "ctx", False)
    through_grad = jnp.sum(exit_adjoint * entry_state, axis=(2, 3))
    second_grads = states_back((first_grads[4], exit_adjoint, through_grad))
    grad_input = (first_grads[0] + second_grads[0]).reshape(
        tokens_here, heads_here * HEAD_DIM
    ) + grad_core * skip_cols
    grad_step = (first_grads[1] + second_grads[1]).reshape(
        tokens_here, heads_here
    ) * jax.nn.sigmoid(shifted)
    grad_b_matrix = (first_grads[2] + second_grads[2]).reshape(tokens_here, groups_here * STATE)
    grad_c_matrix = first_grads[3].reshape(tokens_here, groups_here * STATE)
    return (
        grad_input.astype(jnp.bfloat16),
        grad_gate.astype(jnp.bfloat16),
        grad_step,
        grad_b_matrix,
        grad_c_matrix,
    )


def solution(mesh):
    return jax.shard_map(
        body,
        mesh=mesh,
        in_specs=(
            P("ctx", "head"),
            P("ctx", "head"),
            P("ctx", "head"),
            P("ctx", "head"),
            P("ctx", "head"),
            P("head"),
            P("head"),
            P("head"),
            P("head"),
            P("ctx"),
            P("ctx", "head"),
        ),
        out_specs=(
            P("ctx", "head"),
            P("ctx", "head"),
            P("ctx", "head"),
            P("ctx", "head"),
            P("ctx", "head"),
        ),
        check_vma=False,
    )
```

```python
import jax
import jax.numpy as jnp
from jax import lax
from jax.sharding import PartitionSpec as P

HEAD_DIM = 64
STATE = 128
SPAN = 256


HIGHEST_PRECISION = lax.Precision.HIGHEST
EPSILON = 1e-05


def pack_pair(gain, value):
    rows = value.reshape(-1, value.shape[-1])
    pad = jnp.zeros((8, value.shape[-1]), value.dtype)
    pad = pad.at[0, : gain.size].set(gain.reshape(-1))
    return jnp.concatenate([rows, pad], axis=0)


def unpack_pair(packed, gain, value):
    rows = value.size // value.shape[-1]
    return (
        packed[rows, : gain.size].reshape(gain.shape),
        packed[:rows].reshape(value.shape),
    )


def exclusive_scan(gain, value, axis, forward):
    size = lax.axis_size(axis)
    total = jnp.zeros_like(value)
    total_gain = jnp.ones_like(gain)
    distance = 1
    while distance < size:
        if forward:
            pairs = [(i, i + distance) for i in range(size - distance)]
        else:
            pairs = [(i + distance, i) for i in range(size - distance)]
        moved = lax.ppermute(pack_pair(gain, value), axis, pairs)
        gain_in, value_in = unpack_pair(moved, gain, value)
        total = total + total_gain[..., None, None] * value_in
        distance *= 2
        if distance < size:
            total_gain = total_gain * gain_in
            value = value + gain[..., None, None] * value_in
            gain = gain * gain_in
    return total


def butterfly_sum(value, axis):
    size = lax.axis_size(axis)
    step = 1
    while step < size:
        pairs = [(i, i ^ step) for i in range(size)]
        value = value + lax.ppermute(value, axis, pairs)
        step *= 2
    return value


def span_mix(x_span, dt_span, b_span, c_span, log_cum, segment):
    log_rows = jnp.moveaxis(log_cum, 0, -1)
    spread = log_rows[..., :, None] - log_rows[..., None, :]
    places = jnp.arange(x_span.shape[0], dtype=jnp.int32)
    keep_mask = (
        (places[:, None] >= places[None, :]) & (segment[:, None] == segment[None, :])
    ).astype(jnp.float32)
    masked = jnp.exp(jnp.minimum(spread, 0.0)) * keep_mask
    scores = jnp.einsum("tgn,sgn->gts", c_span, b_span, precision=HIGHEST_PRECISION)
    weights = scores[:, None] * masked * jnp.moveaxis(dt_span, 0, -1)[..., None, :]
    return jnp.einsum("ghts,sghp->tghp", weights, x_span, precision=HIGHEST_PRECISION)


def block_decays(dt_spans, segment, decay_rate):
    log_cum = jnp.cumsum(dt_spans * decay_rate, axis=1)
    closing = segment[:, -1]
    through = jnp.exp(log_cum[:, -1]) * (closing == 0).astype(jnp.float32)[:, None, None]
    return (log_cum, closing, through)


def local_states(x_spans, dt_spans, b_spans, segment, decay_rate):
    log_cum, closing, through = block_decays(dt_spans, segment, decay_rate)
    same_doc = (segment == closing[:, None]).astype(jnp.float32)
    tail_decay = jnp.exp(log_cum[:, -1:] - log_cum) * same_doc[:, :, None, None]
    added_terms = jnp.einsum(
        "kqgh,kqghp,kqgn->kghpn",
        tail_decay * dt_spans,
        x_spans,
        b_spans,
        precision=HIGHEST_PRECISION,
    )

    def advance(carried_pair, item_pair):
        carry_state, product = carried_pair
        decay_now, fresh_state = item_pair
        return (
            (decay_now[..., None, None] * carry_state + fresh_state, product * decay_now),
            carry_state,
        )

    initial = (
        jnp.zeros(added_terms.shape[1:], jnp.float32),
        jnp.ones(through.shape[1:], jnp.float32),
    )
    (final_state, product), starts = lax.scan(advance, initial, (through, added_terms))
    return (starts, final_state, product)


def output_part(x_spans, dt_spans, b_spans, c_spans, segment, decay_rate, starts, entry_state):
    log_cum, closing, through = block_decays(dt_spans, segment, decay_rate)

    def rolling(product, decay_now):
        return (product * decay_now, product)

    _, before = lax.scan(rolling, jnp.ones(through.shape[1:], jnp.float32), through)
    full_start = starts + before[..., None, None] * entry_state[None]
    opened = (segment == 0).astype(jnp.float32)
    entry_decay = jnp.exp(log_cum) * opened[:, :, None, None]
    carried = (
        jnp.einsum("kqgn,kghpn->kqghp", c_spans, full_start, precision=HIGHEST_PRECISION)
        * entry_decay[..., None]
    )
    mix_block = jax.checkpoint(lambda pieces: span_mix(*pieces))
    inner_part = lax.map(mix_block, (x_spans, dt_spans, b_spans, c_spans, log_cum, segment))
    return inner_part + carried


def body(
    ssm_input,
    gate_input,
    step_raw,
    b_matrix,
    c_matrix,
    step_bias,
    log_rate,
    skip_gain,
    norm_weight,
    doc_resets,
    grad_output,
):
    tokens_here = ssm_input.shape[0]
    heads_here = step_raw.shape[1]
    groups_here = b_matrix.shape[1] // STATE
    per_group = heads_here // groups_here
    spans = tokens_here // SPAN
    x_float = ssm_input.astype(jnp.float32)
    gate_float = gate_input.astype(jnp.float32)
    shifted = step_raw + step_bias[None, :]
    step_size = jax.nn.softplus(shifted)
    decay_rate = (-jnp.exp(log_rate)).reshape(groups_here, per_group)
    x_spans = x_float.reshape(spans, SPAN, groups_here, per_group, HEAD_DIM)
    dt_spans = step_size.reshape(spans, SPAN, groups_here, per_group)
    b_spans = b_matrix.astype(jnp.float32).reshape(spans, SPAN, groups_here, STATE)
    c_spans = c_matrix.astype(jnp.float32).reshape(spans, SPAN, groups_here, STATE)
    segment = jnp.cumsum(doc_resets.reshape(spans, SPAN), axis=1, dtype=jnp.int32)

    def states_call(x_value, dt_value, b_value):
        return local_states(x_value, dt_value, b_value, segment, decay_rate)

    (starts, end_local, through_all), states_back = jax.vjp(states_call, x_spans, dt_spans, b_spans)
    entry_state = exclusive_scan(through_all, end_local, "ctx", True)

    def output_call(x_value, dt_value, b_value, c_value, start_value, entry_value):
        return output_part(
            x_value, dt_value, b_value, c_value, segment, decay_rate, start_value, entry_value
        )

    core_part, output_back = jax.vjp(
        output_call, x_spans, dt_spans, b_spans, c_spans, starts, entry_state
    )
    skip_cols = jnp.repeat(skip_gain, HEAD_DIM)[None, :]
    core_out = core_part.reshape(tokens_here, heads_here * HEAD_DIM) + x_float * skip_cols
    gate_sig = jax.nn.sigmoid(gate_float)
    gate_act = gate_float * gate_sig
    gated = core_out * gate_act
    weighted_grad = norm_weight[None, :] * grad_output.astype(jnp.float32)
    norm_width = lax.axis_size("head") * gated.shape[1]
    sums = butterfly_sum(
        jnp.stack([jnp.sum(gated * gated, axis=1), jnp.sum(weighted_grad * gated, axis=1)]),
        "head",
    )
    inv_rms = lax.rsqrt(sums[0] / norm_width + EPSILON)
    normed = gated * inv_rms[:, None]
    product = sums[1] * inv_rms
    grad_gated = inv_rms[:, None] * (weighted_grad - normed * (product / norm_width)[:, None])
    grad_core = grad_gated * gate_act
    grad_gate = grad_gated * core_out * gate_sig * (1.0 + gate_float * (1.0 - gate_sig))
    first_grads = output_back(grad_core.reshape(core_part.shape))
    exit_adjoint = exclusive_scan(through_all, first_grads[5], "ctx", False)
    through_grad = jnp.sum(exit_adjoint * entry_state, axis=(2, 3))
    second_grads = states_back((first_grads[4], exit_adjoint, through_grad))
    grad_input = (first_grads[0] + second_grads[0]).reshape(
        tokens_here, heads_here * HEAD_DIM
    ) + grad_core * skip_cols
    grad_step = (first_grads[1] + second_grads[1]).reshape(
        tokens_here, heads_here
    ) * jax.nn.sigmoid(shifted)
    grad_b_matrix = (first_grads[2] + second_grads[2]).reshape(tokens_here, groups_here * STATE)
    grad_c_matrix = first_grads[3].reshape(tokens_here, groups_here * STATE)
    return (
        grad_input.astype(jnp.bfloat16),
        grad_gate.astype(jnp.bfloat16),
        grad_step,
        grad_b_matrix,
        grad_c_matrix,
    )


def solution(mesh):
    return jax.shard_map(
        body,
        mesh=mesh,
        in_specs=(
            P("ctx", "head"),
            P("ctx", "head"),
            P("ctx", "head"),
            P("ctx", "head"),
            P("ctx", "head"),
            P("head"),
            P("head"),
            P("head"),
            P("head"),
            P("ctx"),
            P("ctx", "head"),
        ),
        out_specs=(
            P("ctx", "head"),
            P("ctx", "head"),
            P("ctx", "head"),
            P("ctx", "head"),
            P("ctx", "head"),
        ),
        check_vma=False,
    )
```

```python
import jax
import jax.numpy as jnp
from jax import lax
from jax.sharding import PartitionSpec as P

HEAD_DIM = 64
STATE = 128
SPAN = 256


HIGHEST_PRECISION = lax.Precision.HIGHEST
EPSILON = 1e-05


def exclusive_scan(gain, value, move, count):
    total = jnp.zeros_like(value)
    total_gain = jnp.ones_like(gain)
    distance = 1
    while distance < count:
        gain_in, value_in = move((gain, value), distance)
        total = total + total_gain[..., None, None] * value_in
        distance *= 2
        if distance < count:
            total_gain = total_gain * gain_in
            value = value + gain[..., None, None] * value_in
            gain = gain * gain_in
    return total


def chip_scan(gain, value, axis, forward):
    size = lax.axis_size(axis)
    index = lax.axis_index(axis)
    place = index if forward else size - 1 - index
    second = place % 2
    is_second = second == 1
    half = value.shape[1] // 2

    def device(p):
        return p if forward else size - 1 - p

    def move(tree, pairs):
        return lax.ppermute(tree, axis, [(device(a), device(b)) for a, b in pairs])

    def pick(array, which):
        return lax.dynamic_slice_in_dim(array, which * half, half, axis=1)

    partners = [(p, p ^ 1) for p in range(size)]
    own_gain, own_value = pick(gain, second), pick(value, second)
    got_gain, got_value = move((pick(gain, 1 - second), pick(value, 1 - second)), partners)
    first_gain = jnp.where(is_second, got_gain, own_gain)
    first_value = jnp.where(is_second, got_value, own_value)
    second_gain = jnp.where(is_second, own_gain, got_gain)
    second_value = jnp.where(is_second, own_value, got_value)
    chip_value = second_gain[..., None, None] * first_value + second_value
    chip_gain = first_gain * second_gain

    def chip_move(tree, distance):
        step = 2 * distance
        return move(tree, [(p, p + step) for p in range(size - step)])

    prefix = exclusive_scan(chip_gain, chip_value, chip_move, size // 2)
    after_first = first_value + first_gain[..., None, None] * prefix
    own_entry = jnp.where(is_second, after_first, prefix)
    got_entry = move(jnp.where(is_second, prefix, after_first), partners)
    return jnp.where(
        is_second,
        jnp.concatenate([got_entry, own_entry], axis=1),
        jnp.concatenate([own_entry, got_entry], axis=1),
    )


def butterfly_sum(value, axis):
    size = lax.axis_size(axis)
    step = 1
    while step < size:
        pairs = [(i, i ^ step) for i in range(size)]
        value = value + lax.ppermute(value, axis, pairs)
        step *= 2
    return value


def span_mix(x_span, dt_span, b_span, c_span, log_cum, segment):
    log_rows = jnp.moveaxis(log_cum, 0, -1)
    spread = log_rows[..., :, None] - log_rows[..., None, :]
    places = jnp.arange(x_span.shape[0], dtype=jnp.int32)
    keep_mask = (
        (places[:, None] >= places[None, :]) & (segment[:, None] == segment[None, :])
    ).astype(jnp.float32)
    masked = jnp.exp(jnp.minimum(spread, 0.0)) * keep_mask
    scores = jnp.einsum("tgn,sgn->gts", c_span, b_span, precision=HIGHEST_PRECISION)
    weights = scores[:, None] * masked * jnp.moveaxis(dt_span, 0, -1)[..., None, :]
    return jnp.einsum("ghts,sghp->tghp", weights, x_span, precision=HIGHEST_PRECISION)


def block_decays(dt_spans, segment, decay_rate):
    log_cum = jnp.cumsum(dt_spans * decay_rate, axis=1)
    closing = segment[:, -1]
    through = jnp.exp(log_cum[:, -1]) * (closing == 0).astype(jnp.float32)[:, None, None]
    return (log_cum, closing, through)


def local_states(x_spans, dt_spans, b_spans, segment, decay_rate):
    log_cum, closing, through = block_decays(dt_spans, segment, decay_rate)
    same_doc = (segment == closing[:, None]).astype(jnp.float32)
    tail_decay = jnp.exp(log_cum[:, -1:] - log_cum) * same_doc[:, :, None, None]
    added_terms = jnp.einsum(
        "kqgh,kqghp,kqgn->kghpn",
        tail_decay * dt_spans,
        x_spans,
        b_spans,
        precision=HIGHEST_PRECISION,
    )

    def advance(carried_pair, item_pair):
        carry_state, product = carried_pair
        decay_now, fresh_state = item_pair
        return (
            (decay_now[..., None, None] * carry_state + fresh_state, product * decay_now),
            carry_state,
        )

    initial = (
        jnp.zeros(added_terms.shape[1:], jnp.float32),
        jnp.ones(through.shape[1:], jnp.float32),
    )
    (final_state, product), starts = lax.scan(advance, initial, (through, added_terms))
    return (starts, final_state, product)


def output_part(x_spans, dt_spans, b_spans, c_spans, segment, decay_rate, starts, entry_state):
    log_cum, closing, through = block_decays(dt_spans, segment, decay_rate)

    def rolling(product, decay_now):
        return (product * decay_now, product)

    _, before = lax.scan(rolling, jnp.ones(through.shape[1:], jnp.float32), through)
    full_start = starts + before[..., None, None] * entry_state[None]
    opened = (segment == 0).astype(jnp.float32)
    entry_decay = jnp.exp(log_cum) * opened[:, :, None, None]
    carried = (
        jnp.einsum("kqgn,kghpn->kqghp", c_spans, full_start, precision=HIGHEST_PRECISION)
        * entry_decay[..., None]
    )
    mix_block = jax.checkpoint(lambda pieces: span_mix(*pieces))
    inner_part = lax.map(mix_block, (x_spans, dt_spans, b_spans, c_spans, log_cum, segment))
    return inner_part + carried


def body(
    ssm_input,
    gate_input,
    step_raw,
    b_matrix,
    c_matrix,
    step_bias,
    log_rate,
    skip_gain,
    norm_weight,
    doc_resets,
    grad_output,
):
    tokens_here = ssm_input.shape[0]
    heads_here = step_raw.shape[1]
    groups_here = b_matrix.shape[1] // STATE
    per_group = heads_here // groups_here
    spans = tokens_here // SPAN
    x_float = ssm_input.astype(jnp.float32)
    gate_float = gate_input.astype(jnp.float32)
    shifted = step_raw + step_bias[None, :]
    step_size = jax.nn.softplus(shifted)
    decay_rate = (-jnp.exp(log_rate)).reshape(groups_here, per_group)
    x_spans = x_float.reshape(spans, SPAN, groups_here, per_group, HEAD_DIM)
    dt_spans = step_size.reshape(spans, SPAN, groups_here, per_group)
    b_spans = b_matrix.astype(jnp.float32).reshape(spans, SPAN, groups_here, STATE)
    c_spans = c_matrix.astype(jnp.float32).reshape(spans, SPAN, groups_here, STATE)
    segment = jnp.cumsum(doc_resets.reshape(spans, SPAN), axis=1, dtype=jnp.int32)

    def states_call(x_value, dt_value, b_value):
        return local_states(x_value, dt_value, b_value, segment, decay_rate)

    (starts, end_local, through_all), states_back = jax.vjp(states_call, x_spans, dt_spans, b_spans)
    entry_state = chip_scan(through_all, end_local, "ctx", True)

    def output_call(x_value, dt_value, b_value, c_value, start_value, entry_value):
        return output_part(
            x_value, dt_value, b_value, c_value, segment, decay_rate, start_value, entry_value
        )

    core_part, output_back = jax.vjp(
        output_call, x_spans, dt_spans, b_spans, c_spans, starts, entry_state
    )
    skip_cols = jnp.repeat(skip_gain, HEAD_DIM)[None, :]
    core_out = core_part.reshape(tokens_here, heads_here * HEAD_DIM) + x_float * skip_cols
    gate_sig = jax.nn.sigmoid(gate_float)
    gate_act = gate_float * gate_sig
    gated = core_out * gate_act
    weighted_grad = norm_weight[None, :] * grad_output.astype(jnp.float32)
    norm_width = lax.axis_size("head") * gated.shape[1]
    sums = butterfly_sum(
        jnp.stack([jnp.sum(gated * gated, axis=1), jnp.sum(weighted_grad * gated, axis=1)]),
        "head",
    )
    inv_rms = lax.rsqrt(sums[0] / norm_width + EPSILON)
    normed = gated * inv_rms[:, None]
    product = sums[1] * inv_rms
    grad_gated = inv_rms[:, None] * (weighted_grad - normed * (product / norm_width)[:, None])
    grad_core = grad_gated * gate_act
    grad_gate = grad_gated * core_out * gate_sig * (1.0 + gate_float * (1.0 - gate_sig))
    first_grads = output_back(grad_core.reshape(core_part.shape))
    exit_adjoint = chip_scan(through_all, first_grads[5], "ctx", False)
    through_grad = jnp.sum(exit_adjoint * entry_state, axis=(2, 3))
    second_grads = states_back((first_grads[4], exit_adjoint, through_grad))
    grad_input = (first_grads[0] + second_grads[0]).reshape(
        tokens_here, heads_here * HEAD_DIM
    ) + grad_core * skip_cols
    grad_step = (first_grads[1] + second_grads[1]).reshape(
        tokens_here, heads_here
    ) * jax.nn.sigmoid(shifted)
    grad_b_matrix = (first_grads[2] + second_grads[2]).reshape(tokens_here, groups_here * STATE)
    grad_c_matrix = first_grads[3].reshape(tokens_here, groups_here * STATE)
    return (
        grad_input.astype(jnp.bfloat16),
        grad_gate.astype(jnp.bfloat16),
        grad_step,
        grad_b_matrix,
        grad_c_matrix,
    )


def solution(mesh):
    return jax.shard_map(
        body,
        mesh=mesh,
        in_specs=(
            P("ctx", "head"),
            P("ctx", "head"),
            P("ctx", "head"),
            P("ctx", "head"),
            P("ctx", "head"),
            P("head"),
            P("head"),
            P("head"),
            P("head"),
            P("ctx"),
            P("ctx", "head"),
        ),
        out_specs=(
            P("ctx", "head"),
            P("ctx", "head"),
            P("ctx", "head"),
            P("ctx", "head"),
            P("ctx", "head"),
        ),
        check_vma=False,
    )
```

```python
import jax
import jax.numpy as jnp
from jax import lax
from jax.sharding import PartitionSpec as P

HEAD_DIM = 64
STATE = 128
SPAN = 256


HIGHEST_PRECISION = lax.Precision.HIGHEST
EPSILON = 1e-05


def exclusive_scan(gain, value, move, count):
    total = jnp.zeros_like(value)
    total_gain = jnp.ones_like(gain)
    distance = 1
    while distance < count:
        gain_in, value_in = move((gain, value), distance)
        total = total + total_gain[..., None, None] * value_in
        distance *= 2
        if distance < count:
            total_gain = total_gain * gain_in
            value = value + gain[..., None, None] * value_in
            gain = gain * gain_in
    return total


def chip_scan(gain, value, axis, forward):
    size = lax.axis_size(axis)
    index = lax.axis_index(axis)
    place = index if forward else size - 1 - index
    second = place % 2
    is_second = second == 1
    half = value.shape[1] // 2

    def device(p):
        return p if forward else size - 1 - p

    def move(tree, pairs):
        return lax.ppermute(tree, axis, [(device(a), device(b)) for a, b in pairs])

    def pick(array, which):
        return lax.dynamic_slice_in_dim(array, which * half, half, axis=1)

    partners = [(p, p ^ 1) for p in range(size)]
    own_gain, own_value = pick(gain, second), pick(value, second)
    got_gain, got_value = move((pick(gain, 1 - second), pick(value, 1 - second)), partners)
    first_gain = jnp.where(is_second, got_gain, own_gain)
    first_value = jnp.where(is_second, got_value, own_value)
    second_gain = jnp.where(is_second, own_gain, got_gain)
    second_value = jnp.where(is_second, own_value, got_value)
    chip_value = second_gain[..., None, None] * first_value + second_value
    chip_gain = first_gain * second_gain

    def chip_move(tree, distance):
        step = 2 * distance
        return move(tree, [(p, p + step) for p in range(size - step)])

    prefix = exclusive_scan(chip_gain, chip_value, chip_move, size // 2)
    after_first = first_value + first_gain[..., None, None] * prefix
    own_entry = jnp.where(is_second, after_first, prefix)
    got_entry = move(jnp.where(is_second, prefix, after_first), partners)
    return jnp.where(
        is_second,
        jnp.concatenate([got_entry, own_entry], axis=1),
        jnp.concatenate([own_entry, got_entry], axis=1),
    )


def head_sum(value, axis):
    size = lax.axis_size(axis)
    spread = jnp.broadcast_to(value[None], (size,) + value.shape)
    return jnp.sum(lax.all_to_all(spread, axis, 0, 0), axis=0)


def span_mix(x_span, dt_span, b_span, c_span, log_cum, segment):
    log_rows = jnp.moveaxis(log_cum, 0, -1)
    spread = log_rows[..., :, None] - log_rows[..., None, :]
    places = jnp.arange(x_span.shape[0], dtype=jnp.int32)
    keep_mask = (
        (places[:, None] >= places[None, :]) & (segment[:, None] == segment[None, :])
    ).astype(jnp.float32)
    masked = jnp.exp(jnp.minimum(spread, 0.0)) * keep_mask
    scores = jnp.einsum("tgn,sgn->gts", c_span, b_span, precision=HIGHEST_PRECISION)
    weights = scores[:, None] * masked * jnp.moveaxis(dt_span, 0, -1)[..., None, :]
    return jnp.einsum("ghts,sghp->tghp", weights, x_span, precision=HIGHEST_PRECISION)


def block_decays(dt_spans, segment, decay_rate):
    log_cum = jnp.cumsum(dt_spans * decay_rate, axis=1)
    closing = segment[:, -1]
    through = jnp.exp(log_cum[:, -1]) * (closing == 0).astype(jnp.float32)[:, None, None]
    return (log_cum, closing, through)


def local_states(x_spans, dt_spans, b_spans, segment, decay_rate):
    log_cum, closing, through = block_decays(dt_spans, segment, decay_rate)
    same_doc = (segment == closing[:, None]).astype(jnp.float32)
    tail_decay = jnp.exp(log_cum[:, -1:] - log_cum) * same_doc[:, :, None, None]
    added_terms = jnp.einsum(
        "kqgh,kqghp,kqgn->kghpn",
        tail_decay * dt_spans,
        x_spans,
        b_spans,
        precision=HIGHEST_PRECISION,
    )

    def advance(carried_pair, item_pair):
        carry_state, product = carried_pair
        decay_now, fresh_state = item_pair
        return (
            (decay_now[..., None, None] * carry_state + fresh_state, product * decay_now),
            carry_state,
        )

    initial = (
        jnp.zeros(added_terms.shape[1:], jnp.float32),
        jnp.ones(through.shape[1:], jnp.float32),
    )
    (final_state, product), starts = lax.scan(advance, initial, (through, added_terms))
    return (starts, final_state, product)


def output_part(x_spans, dt_spans, b_spans, c_spans, segment, decay_rate, starts, entry_state):
    log_cum, closing, through = block_decays(dt_spans, segment, decay_rate)

    def rolling(product, decay_now):
        return (product * decay_now, product)

    _, before = lax.scan(rolling, jnp.ones(through.shape[1:], jnp.float32), through)
    full_start = starts + before[..., None, None] * entry_state[None]
    opened = (segment == 0).astype(jnp.float32)
    entry_decay = jnp.exp(log_cum) * opened[:, :, None, None]
    carried = (
        jnp.einsum("kqgn,kghpn->kqghp", c_spans, full_start, precision=HIGHEST_PRECISION)
        * entry_decay[..., None]
    )
    mix_block = jax.checkpoint(lambda pieces: span_mix(*pieces))
    inner_part = lax.map(mix_block, (x_spans, dt_spans, b_spans, c_spans, log_cum, segment))
    return inner_part + carried


def body(
    ssm_input,
    gate_input,
    step_raw,
    b_matrix,
    c_matrix,
    step_bias,
    log_rate,
    skip_gain,
    norm_weight,
    doc_resets,
    grad_output,
):
    tokens_here = ssm_input.shape[0]
    heads_here = step_raw.shape[1]
    groups_here = b_matrix.shape[1] // STATE
    per_group = heads_here // groups_here
    spans = tokens_here // SPAN
    x_float = ssm_input.astype(jnp.float32)
    gate_float = gate_input.astype(jnp.float32)
    shifted = step_raw + step_bias[None, :]
    step_size = jax.nn.softplus(shifted)
    decay_rate = (-jnp.exp(log_rate)).reshape(groups_here, per_group)
    x_spans = x_float.reshape(spans, SPAN, groups_here, per_group, HEAD_DIM)
    dt_spans = step_size.reshape(spans, SPAN, groups_here, per_group)
    b_spans = b_matrix.astype(jnp.float32).reshape(spans, SPAN, groups_here, STATE)
    c_spans = c_matrix.astype(jnp.float32).reshape(spans, SPAN, groups_here, STATE)
    segment = jnp.cumsum(doc_resets.reshape(spans, SPAN), axis=1, dtype=jnp.int32)

    def states_call(x_value, dt_value, b_value):
        return local_states(x_value, dt_value, b_value, segment, decay_rate)

    (starts, end_local, through_all), states_back = jax.vjp(states_call, x_spans, dt_spans, b_spans)
    entry_state = chip_scan(through_all, end_local, "ctx", True)

    def output_call(x_value, dt_value, b_value, c_value, start_value, entry_value):
        return output_part(
            x_value, dt_value, b_value, c_value, segment, decay_rate, start_value, entry_value
        )

    core_part, output_back = jax.vjp(
        output_call, x_spans, dt_spans, b_spans, c_spans, starts, entry_state
    )
    skip_cols = jnp.repeat(skip_gain, HEAD_DIM)[None, :]
    core_out = core_part.reshape(tokens_here, heads_here * HEAD_DIM) + x_float * skip_cols
    gate_sig = jax.nn.sigmoid(gate_float)
    gate_act = gate_float * gate_sig
    gated = core_out * gate_act
    weighted_grad = norm_weight[None, :] * grad_output.astype(jnp.float32)
    norm_width = lax.axis_size("head") * gated.shape[1]
    sums = head_sum(
        jnp.stack([jnp.sum(gated * gated, axis=1), jnp.sum(weighted_grad * gated, axis=1)]),
        "head",
    )
    inv_rms = lax.rsqrt(sums[0] / norm_width + EPSILON)
    normed = gated * inv_rms[:, None]
    product = sums[1] * inv_rms
    grad_gated = inv_rms[:, None] * (weighted_grad - normed * (product / norm_width)[:, None])
    grad_core = grad_gated * gate_act
    grad_gate = grad_gated * core_out * gate_sig * (1.0 + gate_float * (1.0 - gate_sig))
    first_grads = output_back(grad_core.reshape(core_part.shape))
    exit_adjoint = chip_scan(through_all, first_grads[5], "ctx", False)
    through_grad = jnp.sum(exit_adjoint * entry_state, axis=(2, 3))
    second_grads = states_back((first_grads[4], exit_adjoint, through_grad))
    grad_input = (first_grads[0] + second_grads[0]).reshape(
        tokens_here, heads_here * HEAD_DIM
    ) + grad_core * skip_cols
    grad_step = (first_grads[1] + second_grads[1]).reshape(
        tokens_here, heads_here
    ) * jax.nn.sigmoid(shifted)
    grad_b_matrix = (first_grads[2] + second_grads[2]).reshape(tokens_here, groups_here * STATE)
    grad_c_matrix = first_grads[3].reshape(tokens_here, groups_here * STATE)
    return (
        grad_input.astype(jnp.bfloat16),
        grad_gate.astype(jnp.bfloat16),
        grad_step,
        grad_b_matrix,
        grad_c_matrix,
    )


def solution(mesh):
    return jax.shard_map(
        body,
        mesh=mesh,
        in_specs=(
            P("ctx", "head"),
            P("ctx", "head"),
            P("ctx", "head"),
            P("ctx", "head"),
            P("ctx", "head"),
            P("head"),
            P("head"),
            P("head"),
            P("head"),
            P("ctx"),
            P("ctx", "head"),
        ),
        out_specs=(
            P("ctx", "head"),
            P("ctx", "head"),
            P("ctx", "head"),
            P("ctx", "head"),
            P("ctx", "head"),
        ),
        check_vma=False,
    )
```

```python
import jax
import jax.numpy as jnp
from jax import lax
from jax.sharding import PartitionSpec as P

HEAD_DIM = 64
STATE = 128
SPAN = 256


HIGHEST_PRECISION = lax.Precision.HIGHEST
EPSILON = 1e-05


def exclusive_scan(value, window, move, count):
    total = jnp.zeros_like(value)
    distance = 1
    while distance < count:
        value_in = move(value, distance)
        total = total + window(1 - distance, -1)[..., None, None] * value_in
        if 2 * distance < count:
            value = value + window(1 - distance, 0)[..., None, None] * value_in
        distance *= 2
    return total


def chip_scan(table, value, axis, forward):
    size = lax.axis_size(axis)
    index = lax.axis_index(axis)
    place = index if forward else size - 1 - index
    second = place % 2
    is_second = second == 1
    chip = place // 2
    half = value.shape[1] // 2

    def device(p):
        return p if forward else size - 1 - p

    def move(array, pairs):
        return lax.ppermute(array, axis, [(device(a), device(b)) for a, b in pairs])

    def pick(array, which, axis_at):
        return lax.dynamic_slice_in_dim(array, which * half, half, axis=axis_at)

    ordered = table if forward else table[::-1]
    gains = pick(ordered, second, 2).reshape((size // 2, 2) + ordered.shape[1:2] + (half,))
    first_gain = gains[chip, 0]
    chip_gains = gains[:, 0] * gains[:, 1]
    chips = jnp.arange(size // 2, dtype=jnp.int32)

    def window(low, high):
        inside = (chips >= chip + low) & (chips <= chip + high)
        return jnp.prod(jnp.where(inside[:, None, None], chip_gains, 1.0), axis=0)

    partners = [(p, p ^ 1) for p in range(size)]
    own_value = pick(value, second, 1)
    got_value = move(pick(value, 1 - second, 1), partners)
    first_value = jnp.where(is_second, got_value, own_value)
    second_value = jnp.where(is_second, own_value, got_value)
    chip_value = gains[chip, 1][..., None, None] * first_value + second_value

    def chip_move(array, distance):
        step = 2 * distance
        return move(array, [(p, p + step) for p in range(size - step)])

    prefix = exclusive_scan(chip_value, window, chip_move, size // 2)
    after_first = first_value + first_gain[..., None, None] * prefix
    own_entry = jnp.where(is_second, after_first, prefix)
    got_entry = move(jnp.where(is_second, prefix, after_first), partners)
    return jnp.where(
        is_second,
        jnp.concatenate([got_entry, own_entry], axis=1),
        jnp.concatenate([own_entry, got_entry], axis=1),
    )


def head_sum(value, axis):
    size = lax.axis_size(axis)
    spread = jnp.broadcast_to(value[None], (size,) + value.shape)
    return jnp.sum(lax.all_to_all(spread, axis, 0, 0), axis=0)


def span_mix(x_span, dt_span, b_span, c_span, log_cum, segment):
    log_rows = jnp.moveaxis(log_cum, 0, -1)
    spread = log_rows[..., :, None] - log_rows[..., None, :]
    places = jnp.arange(x_span.shape[0], dtype=jnp.int32)
    keep_mask = (
        (places[:, None] >= places[None, :]) & (segment[:, None] == segment[None, :])
    ).astype(jnp.float32)
    masked = jnp.exp(jnp.minimum(spread, 0.0)) * keep_mask
    scores = jnp.einsum("tgn,sgn->gts", c_span, b_span, precision=HIGHEST_PRECISION)
    weights = scores[:, None] * masked * jnp.moveaxis(dt_span, 0, -1)[..., None, :]
    return jnp.einsum("ghts,sghp->tghp", weights, x_span, precision=HIGHEST_PRECISION)


def block_decays(dt_spans, segment, decay_rate):
    log_cum = jnp.cumsum(dt_spans * decay_rate, axis=1)
    closing = segment[:, -1]
    through = jnp.exp(log_cum[:, -1]) * (closing == 0).astype(jnp.float32)[:, None, None]
    return (log_cum, closing, through)


def local_states(x_spans, dt_spans, b_spans, segment, decay_rate):
    log_cum, closing, through = block_decays(dt_spans, segment, decay_rate)
    same_doc = (segment == closing[:, None]).astype(jnp.float32)
    tail_decay = jnp.exp(log_cum[:, -1:] - log_cum) * same_doc[:, :, None, None]
    added_terms = jnp.einsum(
        "kqgh,kqghp,kqgn->kghpn",
        tail_decay * dt_spans,
        x_spans,
        b_spans,
        precision=HIGHEST_PRECISION,
    )

    def advance(carried_pair, item_pair):
        carry_state, product = carried_pair
        decay_now, fresh_state = item_pair
        return (
            (decay_now[..., None, None] * carry_state + fresh_state, product * decay_now),
            carry_state,
        )

    initial = (
        jnp.zeros(added_terms.shape[1:], jnp.float32),
        jnp.ones(through.shape[1:], jnp.float32),
    )
    (final_state, product), starts = lax.scan(advance, initial, (through, added_terms))
    return (starts, final_state, product)


def output_part(x_spans, dt_spans, b_spans, c_spans, segment, decay_rate, starts, entry_state):
    log_cum, closing, through = block_decays(dt_spans, segment, decay_rate)

    def rolling(product, decay_now):
        return (product * decay_now, product)

    _, before = lax.scan(rolling, jnp.ones(through.shape[1:], jnp.float32), through)
    full_start = starts + before[..., None, None] * entry_state[None]
    opened = (segment == 0).astype(jnp.float32)
    entry_decay = jnp.exp(log_cum) * opened[:, :, None, None]
    carried = (
        jnp.einsum("kqgn,kghpn->kqghp", c_spans, full_start, precision=HIGHEST_PRECISION)
        * entry_decay[..., None]
    )
    mix_block = jax.checkpoint(lambda pieces: span_mix(*pieces))
    inner_part = lax.map(mix_block, (x_spans, dt_spans, b_spans, c_spans, log_cum, segment))
    return inner_part + carried


def body(
    ssm_input,
    gate_input,
    step_raw,
    b_matrix,
    c_matrix,
    step_bias,
    log_rate,
    skip_gain,
    norm_weight,
    doc_resets,
    grad_output,
):
    tokens_here = ssm_input.shape[0]
    heads_here = step_raw.shape[1]
    groups_here = b_matrix.shape[1] // STATE
    per_group = heads_here // groups_here
    spans = tokens_here // SPAN
    x_float = ssm_input.astype(jnp.float32)
    gate_float = gate_input.astype(jnp.float32)
    shifted = step_raw + step_bias[None, :]
    step_size = jax.nn.softplus(shifted)
    decay_rate = (-jnp.exp(log_rate)).reshape(groups_here, per_group)
    x_spans = x_float.reshape(spans, SPAN, groups_here, per_group, HEAD_DIM)
    dt_spans = step_size.reshape(spans, SPAN, groups_here, per_group)
    b_spans = b_matrix.astype(jnp.float32).reshape(spans, SPAN, groups_here, STATE)
    c_spans = c_matrix.astype(jnp.float32).reshape(spans, SPAN, groups_here, STATE)
    segment = jnp.cumsum(doc_resets.reshape(spans, SPAN), axis=1, dtype=jnp.int32)

    def states_call(x_value, dt_value, b_value):
        return local_states(x_value, dt_value, b_value, segment, decay_rate)

    (starts, end_local, through_all), states_back = jax.vjp(states_call, x_spans, dt_spans, b_spans)
    decay_table = lax.all_gather(through_all, "ctx")
    entry_state = chip_scan(decay_table, end_local, "ctx", True)

    def output_call(x_value, dt_value, b_value, c_value, start_value, entry_value):
        return output_part(
            x_value, dt_value, b_value, c_value, segment, decay_rate, start_value, entry_value
        )

    core_part, output_back = jax.vjp(
        output_call, x_spans, dt_spans, b_spans, c_spans, starts, entry_state
    )
    skip_cols = jnp.repeat(skip_gain, HEAD_DIM)[None, :]
    core_out = core_part.reshape(tokens_here, heads_here * HEAD_DIM) + x_float * skip_cols
    gate_sig = jax.nn.sigmoid(gate_float)
    gate_act = gate_float * gate_sig
    gated = core_out * gate_act
    weighted_grad = norm_weight[None, :] * grad_output.astype(jnp.float32)
    norm_width = lax.axis_size("head") * gated.shape[1]
    sums = head_sum(
        jnp.stack([jnp.sum(gated * gated, axis=1), jnp.sum(weighted_grad * gated, axis=1)]),
        "head",
    )
    inv_rms = lax.rsqrt(sums[0] / norm_width + EPSILON)
    normed = gated * inv_rms[:, None]
    product = sums[1] * inv_rms
    grad_gated = inv_rms[:, None] * (weighted_grad - normed * (product / norm_width)[:, None])
    grad_core = grad_gated * gate_act
    grad_gate = grad_gated * core_out * gate_sig * (1.0 + gate_float * (1.0 - gate_sig))
    first_grads = output_back(grad_core.reshape(core_part.shape))
    exit_adjoint = chip_scan(decay_table, first_grads[5], "ctx", False)
    through_grad = jnp.sum(exit_adjoint * entry_state, axis=(2, 3))
    second_grads = states_back((first_grads[4], exit_adjoint, through_grad))
    grad_input = (first_grads[0] + second_grads[0]).reshape(
        tokens_here, heads_here * HEAD_DIM
    ) + grad_core * skip_cols
    grad_step = (first_grads[1] + second_grads[1]).reshape(
        tokens_here, heads_here
    ) * jax.nn.sigmoid(shifted)
    grad_b_matrix = (first_grads[2] + second_grads[2]).reshape(tokens_here, groups_here * STATE)
    grad_c_matrix = first_grads[3].reshape(tokens_here, groups_here * STATE)
    return (
        grad_input.astype(jnp.bfloat16),
        grad_gate.astype(jnp.bfloat16),
        grad_step,
        grad_b_matrix,
        grad_c_matrix,
    )


def solution(mesh):
    return jax.shard_map(
        body,
        mesh=mesh,
        in_specs=(
            P("ctx", "head"),
            P("ctx", "head"),
            P("ctx", "head"),
            P("ctx", "head"),
            P("ctx", "head"),
            P("head"),
            P("head"),
            P("head"),
            P("head"),
            P("ctx"),
            P("ctx", "head"),
        ),
        out_specs=(
            P("ctx", "head"),
            P("ctx", "head"),
            P("ctx", "head"),
            P("ctx", "head"),
            P("ctx", "head"),
        ),
        check_vma=False,
    )
```

```python
import jax
import jax.numpy as jnp
from jax import lax
from jax.sharding import PartitionSpec as P

HEAD_DIM = 64
STATE = 128
SPAN = 256


HIGHEST_PRECISION = lax.Precision.HIGHEST
EPSILON = 1e-05


def exclusive_scan(gain, value, move, count):
    total = jnp.zeros_like(value)
    total_gain = jnp.ones_like(gain)
    distance = 1
    while distance < count:
        gain_in, value_in = move((gain, value), distance)
        total = total + total_gain[..., None, None] * value_in
        distance *= 2
        if distance < count:
            total_gain = total_gain * gain_in
            value = value + gain[..., None, None] * value_in
            gain = gain * gain_in
    return total


def chip_scan(gain, value, axis, forward):
    size = lax.axis_size(axis)
    index = lax.axis_index(axis)
    place = index if forward else size - 1 - index
    second = place % 2
    is_second = second == 1
    half = value.shape[1] // 2

    def device(p):
        return p if forward else size - 1 - p

    def move(tree, pairs):
        return lax.ppermute(tree, axis, [(device(a), device(b)) for a, b in pairs])

    def pick(array, which):
        return lax.dynamic_slice_in_dim(array, which * half, half, axis=1)

    partners = [(p, p ^ 1) for p in range(size)]
    own_gain, own_value = pick(gain, second), pick(value, second)
    got_gain, got_value = move((pick(gain, 1 - second), pick(value, 1 - second)), partners)
    first_gain = jnp.where(is_second, got_gain, own_gain)
    first_value = jnp.where(is_second, got_value, own_value)
    second_gain = jnp.where(is_second, own_gain, got_gain)
    second_value = jnp.where(is_second, own_value, got_value)
    chip_value = second_gain[..., None, None] * first_value + second_value
    chip_gain = first_gain * second_gain

    def chip_move(tree, distance):
        step = 2 * distance
        return move(tree, [(p, p + step) for p in range(size - step)])

    prefix = exclusive_scan(chip_gain, chip_value, chip_move, size // 2)
    after_first = first_value + first_gain[..., None, None] * prefix
    own_entry = jnp.where(is_second, after_first, prefix)
    got_entry = move(jnp.where(is_second, prefix, after_first), partners)
    return jnp.where(
        is_second,
        jnp.concatenate([got_entry, own_entry], axis=1),
        jnp.concatenate([own_entry, got_entry], axis=1),
    )


def head_sum(value, axis):
    size = lax.axis_size(axis)
    spread = jnp.broadcast_to(value[None], (size,) + value.shape)
    return jnp.sum(lax.all_to_all(spread, axis, 0, 0), axis=0)


def split_scan(gain, value, axis, forward, pieces):
    width = value.shape[1] // pieces
    return jnp.concatenate(
        [
            chip_scan(
                gain[:, k * width : (k + 1) * width],
                value[:, k * width : (k + 1) * width],
                axis,
                forward,
            )
            for k in range(pieces)
        ],
        axis=1,
    )


def span_mix(x_span, dt_span, b_span, c_span, log_cum, segment):
    log_rows = jnp.moveaxis(log_cum, 0, -1)
    spread = log_rows[..., :, None] - log_rows[..., None, :]
    places = jnp.arange(x_span.shape[0], dtype=jnp.int32)
    keep_mask = (
        (places[:, None] >= places[None, :]) & (segment[:, None] == segment[None, :])
    ).astype(jnp.float32)
    masked = jnp.exp(jnp.minimum(spread, 0.0)) * keep_mask
    scores = jnp.einsum("tgn,sgn->gts", c_span, b_span, precision=HIGHEST_PRECISION)
    weights = scores[:, None] * masked * jnp.moveaxis(dt_span, 0, -1)[..., None, :]
    return jnp.einsum("ghts,sghp->tghp", weights, x_span, precision=HIGHEST_PRECISION)


def block_decays(dt_spans, segment, decay_rate):
    log_cum = jnp.cumsum(dt_spans * decay_rate, axis=1)
    closing = segment[:, -1]
    through = jnp.exp(log_cum[:, -1]) * (closing == 0).astype(jnp.float32)[:, None, None]
    return (log_cum, closing, through)


def local_states(x_spans, dt_spans, b_spans, segment, decay_rate):
    log_cum, closing, through = block_decays(dt_spans, segment, decay_rate)
    same_doc = (segment == closing[:, None]).astype(jnp.float32)
    tail_decay = jnp.exp(log_cum[:, -1:] - log_cum) * same_doc[:, :, None, None]
    added_terms = jnp.einsum(
        "kqgh,kqghp,kqgn->kghpn",
        tail_decay * dt_spans,
        x_spans,
        b_spans,
        precision=HIGHEST_PRECISION,
    )

    def advance(carried_pair, item_pair):
        carry_state, product = carried_pair
        decay_now, fresh_state = item_pair
        return (
            (decay_now[..., None, None] * carry_state + fresh_state, product * decay_now),
            carry_state,
        )

    initial = (
        jnp.zeros(added_terms.shape[1:], jnp.float32),
        jnp.ones(through.shape[1:], jnp.float32),
    )
    (final_state, product), starts = lax.scan(advance, initial, (through, added_terms))
    return (starts, final_state, product)


def output_part(x_spans, dt_spans, b_spans, c_spans, segment, decay_rate, starts, entry_state):
    log_cum, closing, through = block_decays(dt_spans, segment, decay_rate)

    def rolling(product, decay_now):
        return (product * decay_now, product)

    _, before = lax.scan(rolling, jnp.ones(through.shape[1:], jnp.float32), through)
    full_start = starts + before[..., None, None] * entry_state[None]
    opened = (segment == 0).astype(jnp.float32)
    entry_decay = jnp.exp(log_cum) * opened[:, :, None, None]
    carried = (
        jnp.einsum("kqgn,kghpn->kqghp", c_spans, full_start, precision=HIGHEST_PRECISION)
        * entry_decay[..., None]
    )
    mix_block = jax.checkpoint(lambda pieces: span_mix(*pieces))
    inner_part = lax.map(mix_block, (x_spans, dt_spans, b_spans, c_spans, log_cum, segment))
    return inner_part + carried


def body(
    ssm_input,
    gate_input,
    step_raw,
    b_matrix,
    c_matrix,
    step_bias,
    log_rate,
    skip_gain,
    norm_weight,
    doc_resets,
    grad_output,
):
    tokens_here = ssm_input.shape[0]
    heads_here = step_raw.shape[1]
    groups_here = b_matrix.shape[1] // STATE
    per_group = heads_here // groups_here
    spans = tokens_here // SPAN
    x_float = ssm_input.astype(jnp.float32)
    gate_float = gate_input.astype(jnp.float32)
    shifted = step_raw + step_bias[None, :]
    step_size = jax.nn.softplus(shifted)
    decay_rate = (-jnp.exp(log_rate)).reshape(groups_here, per_group)
    x_spans = x_float.reshape(spans, SPAN, groups_here, per_group, HEAD_DIM)
    dt_spans = step_size.reshape(spans, SPAN, groups_here, per_group)
    b_spans = b_matrix.astype(jnp.float32).reshape(spans, SPAN, groups_here, STATE)
    c_spans = c_matrix.astype(jnp.float32).reshape(spans, SPAN, groups_here, STATE)
    segment = jnp.cumsum(doc_resets.reshape(spans, SPAN), axis=1, dtype=jnp.int32)

    def states_call(x_value, dt_value, b_value):
        return local_states(x_value, dt_value, b_value, segment, decay_rate)

    (starts, end_local, through_all), states_back = jax.vjp(states_call, x_spans, dt_spans, b_spans)
    entry_state = split_scan(through_all, end_local, "ctx", True, 2)

    def output_call(x_value, dt_value, b_value, c_value, start_value, entry_value):
        return output_part(
            x_value, dt_value, b_value, c_value, segment, decay_rate, start_value, entry_value
        )

    core_part, output_back = jax.vjp(
        output_call, x_spans, dt_spans, b_spans, c_spans, starts, entry_state
    )
    skip_cols = jnp.repeat(skip_gain, HEAD_DIM)[None, :]
    core_out = core_part.reshape(tokens_here, heads_here * HEAD_DIM) + x_float * skip_cols
    gate_sig = jax.nn.sigmoid(gate_float)
    gate_act = gate_float * gate_sig
    gated = core_out * gate_act
    weighted_grad = norm_weight[None, :] * grad_output.astype(jnp.float32)
    norm_width = lax.axis_size("head") * gated.shape[1]
    sums = head_sum(
        jnp.stack([jnp.sum(gated * gated, axis=1), jnp.sum(weighted_grad * gated, axis=1)]),
        "head",
    )
    inv_rms = lax.rsqrt(sums[0] / norm_width + EPSILON)
    normed = gated * inv_rms[:, None]
    product = sums[1] * inv_rms
    grad_gated = inv_rms[:, None] * (weighted_grad - normed * (product / norm_width)[:, None])
    grad_core = grad_gated * gate_act
    grad_gate = grad_gated * core_out * gate_sig * (1.0 + gate_float * (1.0 - gate_sig))
    first_grads = output_back(grad_core.reshape(core_part.shape))
    exit_adjoint = split_scan(through_all, first_grads[5], "ctx", False, 2)
    through_grad = jnp.sum(exit_adjoint * entry_state, axis=(2, 3))
    second_grads = states_back((first_grads[4], exit_adjoint, through_grad))
    grad_input = (first_grads[0] + second_grads[0]).reshape(
        tokens_here, heads_here * HEAD_DIM
    ) + grad_core * skip_cols
    grad_step = (first_grads[1] + second_grads[1]).reshape(
        tokens_here, heads_here
    ) * jax.nn.sigmoid(shifted)
    grad_b_matrix = (first_grads[2] + second_grads[2]).reshape(tokens_here, groups_here * STATE)
    grad_c_matrix = first_grads[3].reshape(tokens_here, groups_here * STATE)
    return (
        grad_input.astype(jnp.bfloat16),
        grad_gate.astype(jnp.bfloat16),
        grad_step,
        grad_b_matrix,
        grad_c_matrix,
    )


def solution(mesh):
    return jax.shard_map(
        body,
        mesh=mesh,
        in_specs=(
            P("ctx", "head"),
            P("ctx", "head"),
            P("ctx", "head"),
            P("ctx", "head"),
            P("ctx", "head"),
            P("head"),
            P("head"),
            P("head"),
            P("head"),
            P("ctx"),
            P("ctx", "head"),
        ),
        out_specs=(
            P("ctx", "head"),
            P("ctx", "head"),
            P("ctx", "head"),
            P("ctx", "head"),
            P("ctx", "head"),
        ),
        check_vma=False,
    )
```

```python
import jax
import jax.numpy as jnp
from jax import lax
from jax.sharding import PartitionSpec as P

HEAD_DIM = 64
STATE = 128
SPAN = 256


HIGHEST_PRECISION = lax.Precision.HIGHEST
EPSILON = 1e-05


def exclusive_scan(gain, value, move, count):
    total = jnp.zeros_like(value)
    total_gain = jnp.ones_like(gain)
    distance = 1
    while distance < count:
        gain_in, value_in = move((gain, value), distance)
        total = total + total_gain[..., None, None] * value_in
        distance *= 2
        if distance < count:
            total_gain = total_gain * gain_in
            value = value + gain[..., None, None] * value_in
            gain = gain * gain_in
    return total


def chip_scan(gain, value, axis, forward):
    size = lax.axis_size(axis)
    index = lax.axis_index(axis)
    place = index if forward else size - 1 - index
    second = place % 2
    is_second = second == 1
    half = value.shape[1] // 2

    def device(p):
        return p if forward else size - 1 - p

    def move(tree, pairs):
        return lax.ppermute(tree, axis, [(device(a), device(b)) for a, b in pairs])

    def pick(array, which):
        return lax.dynamic_slice_in_dim(array, which * half, half, axis=1)

    partners = [(p, p ^ 1) for p in range(size)]
    own_gain, own_value = pick(gain, second), pick(value, second)
    got_gain, got_value = move((pick(gain, 1 - second), pick(value, 1 - second)), partners)
    first_gain = jnp.where(is_second, got_gain, own_gain)
    first_value = jnp.where(is_second, got_value, own_value)
    second_gain = jnp.where(is_second, own_gain, got_gain)
    second_value = jnp.where(is_second, own_value, got_value)
    chip_value = second_gain[..., None, None] * first_value + second_value
    chip_gain = first_gain * second_gain

    def chip_move(tree, distance):
        step = 2 * distance
        return move(tree, [(p, p + step) for p in range(size - step)])

    prefix = exclusive_scan(chip_gain, chip_value, chip_move, size // 2)
    after_first = first_value + first_gain[..., None, None] * prefix
    own_entry = jnp.where(is_second, after_first, prefix)
    got_entry = move(jnp.where(is_second, prefix, after_first), partners)
    return jnp.where(
        is_second,
        jnp.concatenate([got_entry, own_entry], axis=1),
        jnp.concatenate([own_entry, got_entry], axis=1),
    )


def head_sum(value, axis):
    size = lax.axis_size(axis)
    spread = jnp.broadcast_to(value[None], (size,) + value.shape)
    return jnp.sum(lax.all_to_all(spread, axis, 0, 0), axis=0)


def span_mix(x_span, dt_span, b_span, c_span, log_cum, segment):
    log_rows = jnp.moveaxis(log_cum, 0, -1)
    spread = log_rows[..., :, None] - log_rows[..., None, :]
    places = jnp.arange(x_span.shape[0], dtype=jnp.int32)
    keep_mask = (
        (places[:, None] >= places[None, :]) & (segment[:, None] == segment[None, :])
    ).astype(jnp.float32)
    masked = jnp.exp(jnp.minimum(spread, 0.0)) * keep_mask
    scores = jnp.einsum("tgn,sgn->gts", c_span, b_span, precision=HIGHEST_PRECISION)
    weights = scores[:, None] * masked * jnp.moveaxis(dt_span, 0, -1)[..., None, :]
    return jnp.einsum("ghts,sghp->tghp", weights, x_span, precision=HIGHEST_PRECISION)


def block_decays(dt_spans, segment, decay_rate):
    log_cum = jnp.cumsum(dt_spans * decay_rate, axis=1)
    closing = segment[:, -1]
    through = jnp.exp(log_cum[:, -1]) * (closing == 0).astype(jnp.float32)[:, None, None]
    return (log_cum, closing, through)


def local_states(x_spans, dt_spans, b_spans, segment, decay_rate):
    log_cum, closing, through = block_decays(dt_spans, segment, decay_rate)
    same_doc = (segment == closing[:, None]).astype(jnp.float32)
    tail_decay = jnp.exp(log_cum[:, -1:] - log_cum) * same_doc[:, :, None, None]
    added_terms = jnp.einsum(
        "kqgh,kqghp,kqgn->kghpn",
        tail_decay * dt_spans,
        x_spans,
        b_spans,
        precision=HIGHEST_PRECISION,
    )

    def advance(carried_pair, item_pair):
        carry_state, product = carried_pair
        decay_now, fresh_state = item_pair
        return (
            (decay_now[..., None, None] * carry_state + fresh_state, product * decay_now),
            carry_state,
        )

    initial = (
        jnp.zeros(added_terms.shape[1:], jnp.float32),
        jnp.ones(through.shape[1:], jnp.float32),
    )
    (final_state, product), starts = lax.scan(advance, initial, (through, added_terms))
    return (starts, final_state, product)


def output_part(x_spans, dt_spans, b_spans, c_spans, segment, decay_rate, starts, entry_state):
    log_cum, closing, through = block_decays(dt_spans, segment, decay_rate)

    def rolling(product, decay_now):
        return (product * decay_now, product)

    _, before = lax.scan(rolling, jnp.ones(through.shape[1:], jnp.float32), through)
    full_start = starts + before[..., None, None] * entry_state[None]
    opened = (segment == 0).astype(jnp.float32)
    entry_decay = jnp.exp(log_cum) * opened[:, :, None, None]
    carried = (
        jnp.einsum("kqgn,kghpn->kqghp", c_spans, full_start, precision=HIGHEST_PRECISION)
        * entry_decay[..., None]
    )
    mix_block = lambda pieces: span_mix(*pieces)
    inner_part = lax.map(mix_block, (x_spans, dt_spans, b_spans, c_spans, log_cum, segment))
    return inner_part + carried


def body(
    ssm_input,
    gate_input,
    step_raw,
    b_matrix,
    c_matrix,
    step_bias,
    log_rate,
    skip_gain,
    norm_weight,
    doc_resets,
    grad_output,
):
    tokens_here = ssm_input.shape[0]
    heads_here = step_raw.shape[1]
    groups_here = b_matrix.shape[1] // STATE
    per_group = heads_here // groups_here
    spans = tokens_here // SPAN
    x_float = ssm_input.astype(jnp.float32)
    gate_float = gate_input.astype(jnp.float32)
    shifted = step_raw + step_bias[None, :]
    step_size = jax.nn.softplus(shifted)
    decay_rate = (-jnp.exp(log_rate)).reshape(groups_here, per_group)
    x_spans = x_float.reshape(spans, SPAN, groups_here, per_group, HEAD_DIM)
    dt_spans = step_size.reshape(spans, SPAN, groups_here, per_group)
    b_spans = b_matrix.astype(jnp.float32).reshape(spans, SPAN, groups_here, STATE)
    c_spans = c_matrix.astype(jnp.float32).reshape(spans, SPAN, groups_here, STATE)
    segment = jnp.cumsum(doc_resets.reshape(spans, SPAN), axis=1, dtype=jnp.int32)

    def states_call(x_value, dt_value, b_value):
        return local_states(x_value, dt_value, b_value, segment, decay_rate)

    (starts, end_local, through_all), states_back = jax.vjp(states_call, x_spans, dt_spans, b_spans)
    entry_state = chip_scan(through_all, end_local, "ctx", True)

    def output_call(x_value, dt_value, b_value, c_value, start_value, entry_value):
        return output_part(
            x_value, dt_value, b_value, c_value, segment, decay_rate, start_value, entry_value
        )

    core_part, output_back = jax.vjp(
        output_call, x_spans, dt_spans, b_spans, c_spans, starts, entry_state
    )
    skip_cols = jnp.repeat(skip_gain, HEAD_DIM)[None, :]
    core_out = core_part.reshape(tokens_here, heads_here * HEAD_DIM) + x_float * skip_cols
    gate_sig = jax.nn.sigmoid(gate_float)
    gate_act = gate_float * gate_sig
    gated = core_out * gate_act
    weighted_grad = norm_weight[None, :] * grad_output.astype(jnp.float32)
    norm_width = lax.axis_size("head") * gated.shape[1]
    sums = head_sum(
        jnp.stack([jnp.sum(gated * gated, axis=1), jnp.sum(weighted_grad * gated, axis=1)]),
        "head",
    )
    inv_rms = lax.rsqrt(sums[0] / norm_width + EPSILON)
    normed = gated * inv_rms[:, None]
    product = sums[1] * inv_rms
    grad_gated = inv_rms[:, None] * (weighted_grad - normed * (product / norm_width)[:, None])
    grad_core = grad_gated * gate_act
    grad_gate = grad_gated * core_out * gate_sig * (1.0 + gate_float * (1.0 - gate_sig))
    first_grads = output_back(grad_core.reshape(core_part.shape))
    exit_adjoint = chip_scan(through_all, first_grads[5], "ctx", False)
    through_grad = jnp.sum(exit_adjoint * entry_state, axis=(2, 3))
    second_grads = states_back((first_grads[4], exit_adjoint, through_grad))
    grad_input = (first_grads[0] + second_grads[0]).reshape(
        tokens_here, heads_here * HEAD_DIM
    ) + grad_core * skip_cols
    grad_step = (first_grads[1] + second_grads[1]).reshape(
        tokens_here, heads_here
    ) * jax.nn.sigmoid(shifted)
    grad_b_matrix = (first_grads[2] + second_grads[2]).reshape(tokens_here, groups_here * STATE)
    grad_c_matrix = first_grads[3].reshape(tokens_here, groups_here * STATE)
    return (
        grad_input.astype(jnp.bfloat16),
        grad_gate.astype(jnp.bfloat16),
        grad_step,
        grad_b_matrix,
        grad_c_matrix,
    )


def solution(mesh):
    return jax.shard_map(
        body,
        mesh=mesh,
        in_specs=(
            P("ctx", "head"),
            P("ctx", "head"),
            P("ctx", "head"),
            P("ctx", "head"),
            P("ctx", "head"),
            P("head"),
            P("head"),
            P("head"),
            P("head"),
            P("ctx"),
            P("ctx", "head"),
        ),
        out_specs=(
            P("ctx", "head"),
            P("ctx", "head"),
            P("ctx", "head"),
            P("ctx", "head"),
            P("ctx", "head"),
        ),
        check_vma=False,
    )
```

```python
import jax
import jax.numpy as jnp
from jax import lax
from jax.sharding import PartitionSpec as P


HEAD_DIM = 64
STATE = 128
SPAN = 256


HIGHEST_PRECISION = lax.Precision.HIGHEST
EPSILON = 1e-05


def exclusive_scan(gain, value, move, count):
    total = jnp.zeros_like(value)
    total_gain = jnp.ones_like(gain)
    distance = 1
    while distance < count:
        gain_in, value_in = move((gain, value), distance)
        total = total + total_gain[..., None, None] * value_in
        distance *= 2
        if distance < count:
            total_gain = total_gain * gain_in
            value = value + gain[..., None, None] * value_in
            gain = gain * gain_in
    return total


def chip_scan(gain, value, axis, forward):
    size = lax.axis_size(axis)
    index = lax.axis_index(axis)
    place = index if forward else size - 1 - index
    second = place % 2
    is_second = second == 1
    half = value.shape[1] // 2

    def device(p):
        return p if forward else size - 1 - p

    def move(tree, pairs):
        return lax.ppermute(tree, axis, [(device(a), device(b)) for a, b in pairs])

    def pick(array, which):
        return lax.dynamic_slice_in_dim(array, which * half, half, axis=1)

    partners = [(p, p ^ 1) for p in range(size)]
    own_gain, own_value = pick(gain, second), pick(value, second)
    got_gain, got_value = move((pick(gain, 1 - second), pick(value, 1 - second)), partners)
    first_gain = jnp.where(is_second, got_gain, own_gain)
    first_value = jnp.where(is_second, got_value, own_value)
    second_gain = jnp.where(is_second, own_gain, got_gain)
    second_value = jnp.where(is_second, own_value, got_value)
    chip_value = second_gain[..., None, None] * first_value + second_value
    chip_gain = first_gain * second_gain

    def chip_move(tree, distance):
        step = 2 * distance
        return move(tree, [(p, p + step) for p in range(size - step)])

    prefix = exclusive_scan(chip_gain, chip_value, chip_move, size // 2)
    after_first = first_value + first_gain[..., None, None] * prefix
    own_entry = jnp.where(is_second, after_first, prefix)
    got_entry = move(jnp.where(is_second, prefix, after_first), partners)
    return jnp.where(
        is_second,
        jnp.concatenate([got_entry, own_entry], axis=1),
        jnp.concatenate([own_entry, got_entry], axis=1),
    )


def head_sum(value, axis):
    size = lax.axis_size(axis)
    spread = jnp.broadcast_to(value[None], (size,) + value.shape)
    return jnp.sum(lax.all_to_all(spread, axis, 0, 0), axis=0)


def span_mix(x_span, dt_span, b_span, c_span, log_cum, segment):
    log_rows = jnp.moveaxis(log_cum, 0, -1)
    spread = log_rows[..., :, None] - log_rows[..., None, :]
    places = jnp.arange(x_span.shape[0], dtype=jnp.int32)
    keep_mask = (
        (places[:, None] >= places[None, :]) & (segment[:, None] == segment[None, :])
    ).astype(jnp.float32)
    masked = jnp.exp(jnp.minimum(spread, 0.0)) * keep_mask
    scores = jnp.einsum("tgn,sgn->gts", c_span, b_span, precision=HIGHEST_PRECISION)
    weights = scores[:, None] * masked * jnp.moveaxis(dt_span, 0, -1)[..., None, :]
    return jnp.einsum("ghts,sghp->tghp", weights, x_span, precision=HIGHEST_PRECISION)


def block_decays(dt_spans, segment, decay_rate):
    log_cum = jnp.cumsum(dt_spans * decay_rate, axis=1)
    closing = segment[:, -1]
    through = jnp.exp(log_cum[:, -1]) * (closing == 0).astype(jnp.float32)[:, None, None]
    return (log_cum, closing, through)


def local_states(x_spans, dt_spans, b_spans, segment, decay_rate):
    log_cum, closing, through = block_decays(dt_spans, segment, decay_rate)
    same_doc = (segment == closing[:, None]).astype(jnp.float32)
    tail_decay = jnp.exp(log_cum[:, -1:] - log_cum) * same_doc[:, :, None, None]
    added_terms = jnp.einsum(
        "kqgh,kqghp,kqgn->kghpn",
        tail_decay * dt_spans,
        x_spans,
        b_spans,
        precision=HIGHEST_PRECISION,
    )

    def advance(carried_pair, item_pair):
        carry_state, product = carried_pair
        decay_now, fresh_state = item_pair
        return (
            (decay_now[..., None, None] * carry_state + fresh_state, product * decay_now),
            carry_state,
        )

    initial = (
        jnp.zeros(added_terms.shape[1:], jnp.float32),
        jnp.ones(through.shape[1:], jnp.float32),
    )
    (final_state, product), starts = lax.scan(advance, initial, (through, added_terms))
    return (starts, final_state, product)


def output_part(x_spans, dt_spans, b_spans, c_spans, segment, decay_rate, starts, entry_state):
    log_cum, _, through = block_decays(dt_spans, segment, decay_rate)

    def rolling(product, decay_now):
        return (product * decay_now, product)

    _, before = lax.scan(rolling, jnp.ones(through.shape[1:], jnp.float32), through)
    full_start = starts + before[..., None, None] * entry_state[None]
    opened = (segment == 0).astype(jnp.float32)
    entry_decay = jnp.exp(log_cum) * opened[:, :, None, None]
    carried = (
        jnp.einsum("kqgn,kghpn->kqghp", c_spans, full_start, precision=HIGHEST_PRECISION)
        * entry_decay[..., None]
    )
    mix_block = lambda pieces: span_mix(*pieces)
    inner_part = lax.map(mix_block, (x_spans, dt_spans, b_spans, c_spans, log_cum, segment))
    return inner_part + carried


def layer_body(
    ssm_input,
    gate_input,
    step_raw,
    b_matrix,
    c_matrix,
    step_bias,
    log_rate,
    skip_gain,
    norm_weight,
    doc_resets,
    grad_output,
):
    tokens_here = ssm_input.shape[0]
    heads_here = step_raw.shape[1]
    groups_here = b_matrix.shape[1] // STATE
    per_group = heads_here // groups_here
    spans = tokens_here // SPAN
    x_float = ssm_input.astype(jnp.float32)
    gate_float = gate_input.astype(jnp.float32)
    shifted = step_raw + step_bias[None, :]
    step_size = jax.nn.softplus(shifted)
    decay_rate = (-jnp.exp(log_rate)).reshape(groups_here, per_group)
    x_spans = x_float.reshape(spans, SPAN, groups_here, per_group, HEAD_DIM)
    dt_spans = step_size.reshape(spans, SPAN, groups_here, per_group)
    b_spans = b_matrix.astype(jnp.float32).reshape(spans, SPAN, groups_here, STATE)
    c_spans = c_matrix.astype(jnp.float32).reshape(spans, SPAN, groups_here, STATE)
    segment = jnp.cumsum(doc_resets.reshape(spans, SPAN), axis=1, dtype=jnp.int32)

    def states_call(x_value, dt_value, b_value):
        return local_states(x_value, dt_value, b_value, segment, decay_rate)

    (starts, end_local, through_all), states_back = jax.vjp(states_call, x_spans, dt_spans, b_spans)
    entry_state = chip_scan(through_all, end_local, "ctx", True)

    def output_call(x_value, dt_value, b_value, c_value, start_value, entry_value):
        return output_part(
            x_value, dt_value, b_value, c_value, segment, decay_rate, start_value, entry_value
        )

    core_part, output_back = jax.vjp(
        output_call, x_spans, dt_spans, b_spans, c_spans, starts, entry_state
    )
    skip_cols = jnp.repeat(skip_gain, HEAD_DIM)[None, :]
    core_out = core_part.reshape(tokens_here, heads_here * HEAD_DIM) + x_float * skip_cols
    gate_sig = jax.nn.sigmoid(gate_float)
    gate_act = gate_float * gate_sig
    gated = core_out * gate_act
    weighted_grad = norm_weight[None, :] * grad_output.astype(jnp.float32)
    norm_width = lax.axis_size("head") * gated.shape[1]
    sums = head_sum(
        jnp.stack([jnp.sum(gated * gated, axis=1), jnp.sum(weighted_grad * gated, axis=1)]),
        "head",
    )
    inv_rms = lax.rsqrt(sums[0] / norm_width + EPSILON)
    normed = gated * inv_rms[:, None]
    product = sums[1] * inv_rms
    grad_gated = inv_rms[:, None] * (weighted_grad - normed * (product / norm_width)[:, None])
    grad_core = grad_gated * gate_act
    grad_gate = grad_gated * core_out * gate_sig * (1.0 + gate_float * (1.0 - gate_sig))
    first_grads = output_back(grad_core.reshape(core_part.shape))
    first_grads = tuple(
        lax.optimization_barrier(part) if k < 4 else part for k, part in enumerate(first_grads)
    )
    exit_adjoint = chip_scan(through_all, first_grads[5], "ctx", False)
    through_grad = jnp.sum(exit_adjoint * entry_state, axis=(2, 3))
    second_grads = states_back((first_grads[4], exit_adjoint, through_grad))
    grad_input = (first_grads[0] + second_grads[0]).reshape(
        tokens_here, heads_here * HEAD_DIM
    ) + grad_core * skip_cols
    grad_step = (first_grads[1] + second_grads[1]).reshape(
        tokens_here, heads_here
    ) * jax.nn.sigmoid(shifted)
    grad_b_matrix = (first_grads[2] + second_grads[2]).reshape(tokens_here, groups_here * STATE)
    grad_c_matrix = first_grads[3].reshape(tokens_here, groups_here * STATE)
    return (
        grad_input.astype(jnp.bfloat16),
        grad_gate.astype(jnp.bfloat16),
        grad_step,
        grad_b_matrix,
        grad_c_matrix,
    )


def solution(mesh):
    return jax.shard_map(
        layer_body,
        mesh=mesh,
        in_specs=(
            P("ctx", "head"),
            P("ctx", "head"),
            P("ctx", "head"),
            P("ctx", "head"),
            P("ctx", "head"),
            P("head"),
            P("head"),
            P("head"),
            P("head"),
            P("ctx"),
            P("ctx", "head"),
        ),
        out_specs=(
            P("ctx", "head"),
            P("ctx", "head"),
            P("ctx", "head"),
            P("ctx", "head"),
            P("ctx", "head"),
        ),
        check_vma=False,
    )
```

```python
import jax
import jax.numpy as jnp
from jax import lax
from jax.sharding import PartitionSpec as P


HEAD_DIM = 64
STATE = 128
SPAN = 256


HIGHEST_PRECISION = lax.Precision.HIGHEST
EPSILON = 1e-05


def exclusive_scan(gain, value, move, count):
    total = jnp.zeros_like(value)
    total_gain = jnp.ones_like(gain)
    distance = 1
    while distance < count:
        gain_in, value_in = move((gain, value), distance)
        total = total + total_gain[..., None, None] * value_in
        distance *= 2
        if distance < count:
            total_gain = total_gain * gain_in
            value = value + gain[..., None, None] * value_in
            gain = gain * gain_in
    return total


def chip_scan(gain, value, axis, forward):
    size = lax.axis_size(axis)
    index = lax.axis_index(axis)
    place = index if forward else size - 1 - index
    second = place % 2
    is_second = second == 1
    half = value.shape[1] // 2

    def device(p):
        return p if forward else size - 1 - p

    def move(tree, pairs):
        return lax.ppermute(tree, axis, [(device(a), device(b)) for a, b in pairs])

    def pick(array, which):
        return lax.dynamic_slice_in_dim(array, which * half, half, axis=1)

    partners = [(p, p ^ 1) for p in range(size)]
    own_gain, own_value = pick(gain, second), pick(value, second)
    got_gain, got_value = move((pick(gain, 1 - second), pick(value, 1 - second)), partners)
    first_gain = jnp.where(is_second, got_gain, own_gain)
    first_value = jnp.where(is_second, got_value, own_value)
    second_gain = jnp.where(is_second, own_gain, got_gain)
    second_value = jnp.where(is_second, own_value, got_value)
    chip_value = second_gain[..., None, None] * first_value + second_value
    chip_gain = first_gain * second_gain

    def chip_move(tree, distance):
        step = 2 * distance
        return move(tree, [(p, p + step) for p in range(size - step)])

    prefix = exclusive_scan(chip_gain, chip_value, chip_move, size // 2)
    after_first = first_value + first_gain[..., None, None] * prefix
    own_entry = jnp.where(is_second, after_first, prefix)
    got_entry = move(jnp.where(is_second, prefix, after_first), partners)
    return jnp.where(
        is_second,
        jnp.concatenate([got_entry, own_entry], axis=1),
        jnp.concatenate([own_entry, got_entry], axis=1),
    )


def head_sum(value, axis):
    size = lax.axis_size(axis)
    spread = jnp.broadcast_to(value[None], (size,) + value.shape)
    return jnp.sum(lax.all_to_all(spread, axis, 0, 0), axis=0)


def span_mix(x_span, dt_span, b_span, c_span, log_cum, segment):
    log_rows = jnp.moveaxis(log_cum, 0, -1)
    spread = log_rows[..., :, None] - log_rows[..., None, :]
    places = jnp.arange(x_span.shape[0], dtype=jnp.int32)
    keep_mask = (
        (places[:, None] >= places[None, :]) & (segment[:, None] == segment[None, :])
    ).astype(jnp.float32)
    masked = jnp.exp(jnp.minimum(spread, 0.0)) * keep_mask
    scores = jnp.einsum("tgn,sgn->gts", c_span, b_span, precision=HIGHEST_PRECISION)
    weights = scores[:, None] * masked * jnp.moveaxis(dt_span, 0, -1)[..., None, :]
    return jnp.einsum("ghts,sghp->tghp", weights, x_span, precision=HIGHEST_PRECISION)


def block_decays(dt_spans, segment, decay_rate):
    length = dt_spans.shape[1]
    places = jnp.arange(length, dtype=jnp.int32)
    lower = (places[:, None] >= places[None, :]).astype(jnp.float32)
    log_cum = jnp.einsum(
        "qs,ksgh->kqgh", lower, dt_spans * decay_rate, precision=HIGHEST_PRECISION
    )
    closing = segment[:, -1]
    through = jnp.exp(log_cum[:, -1]) * (closing == 0).astype(jnp.float32)[:, None, None]
    return (log_cum, closing, through)


def local_states(x_spans, dt_spans, b_spans, segment, decay_rate):
    log_cum, closing, through = block_decays(dt_spans, segment, decay_rate)
    same_doc = (segment == closing[:, None]).astype(jnp.float32)
    tail_decay = jnp.exp(log_cum[:, -1:] - log_cum) * same_doc[:, :, None, None]
    added_terms = jnp.einsum(
        "kqgh,kqghp,kqgn->kghpn",
        tail_decay * dt_spans,
        x_spans,
        b_spans,
        precision=HIGHEST_PRECISION,
    )

    def advance(carried_pair, item_pair):
        carry_state, product = carried_pair
        decay_now, fresh_state = item_pair
        return (
            (decay_now[..., None, None] * carry_state + fresh_state, product * decay_now),
            carry_state,
        )

    initial = (
        jnp.zeros(added_terms.shape[1:], jnp.float32),
        jnp.ones(through.shape[1:], jnp.float32),
    )
    (final_state, product), starts = lax.scan(advance, initial, (through, added_terms))
    return (starts, final_state, product)


def output_part(x_spans, dt_spans, b_spans, c_spans, segment, decay_rate, starts, entry_state):
    log_cum, _, through = block_decays(dt_spans, segment, decay_rate)

    def rolling(product, decay_now):
        return (product * decay_now, product)

    _, before = lax.scan(rolling, jnp.ones(through.shape[1:], jnp.float32), through)
    full_start = starts + before[..., None, None] * entry_state[None]
    opened = (segment == 0).astype(jnp.float32)
    entry_decay = jnp.exp(log_cum) * opened[:, :, None, None]
    carried = (
        jnp.einsum("kqgn,kghpn->kqghp", c_spans, full_start, precision=HIGHEST_PRECISION)
        * entry_decay[..., None]
    )
    mix_block = lambda pieces: span_mix(*pieces)
    inner_part = lax.map(mix_block, (x_spans, dt_spans, b_spans, c_spans, log_cum, segment))
    inner_part = lax.optimization_barrier(inner_part)
    return inner_part + carried


def layer_body(
    ssm_input,
    gate_input,
    step_raw,
    b_matrix,
    c_matrix,
    step_bias,
    log_rate,
    skip_gain,
    norm_weight,
    doc_resets,
    grad_output,
):
    tokens_here = ssm_input.shape[0]
    heads_here = step_raw.shape[1]
    groups_here = b_matrix.shape[1] // STATE
    per_group = heads_here // groups_here
    spans = tokens_here // SPAN
    x_float = ssm_input.astype(jnp.float32)
    gate_float = gate_input.astype(jnp.float32)
    shifted = step_raw + step_bias[None, :]
    step_size = jax.nn.softplus(shifted)
    decay_rate = (-jnp.exp(log_rate)).reshape(groups_here, per_group)
    x_spans = x_float.reshape(spans, SPAN, groups_here, per_group, HEAD_DIM)
    dt_spans = step_size.reshape(spans, SPAN, groups_here, per_group)
    b_spans = b_matrix.astype(jnp.float32).reshape(spans, SPAN, groups_here, STATE)
    c_spans = c_matrix.astype(jnp.float32).reshape(spans, SPAN, groups_here, STATE)
    segment = jnp.cumsum(doc_resets.reshape(spans, SPAN), axis=1, dtype=jnp.int32)

    def states_call(x_value, dt_value, b_value):
        return local_states(x_value, dt_value, b_value, segment, decay_rate)

    (starts, end_local, through_all), states_back = jax.vjp(states_call, x_spans, dt_spans, b_spans)
    entry_state = chip_scan(through_all, end_local, "ctx", True)

    def output_call(x_value, dt_value, b_value, c_value, start_value, entry_value):
        return output_part(
            x_value, dt_value, b_value, c_value, segment, decay_rate, start_value, entry_value
        )

    core_part, output_back = jax.vjp(
        output_call, x_spans, dt_spans, b_spans, c_spans, starts, entry_state
    )
    skip_cols = jnp.repeat(skip_gain, HEAD_DIM)[None, :]
    core_out = core_part.reshape(tokens_here, heads_here * HEAD_DIM) + x_float * skip_cols
    gate_sig = jax.nn.sigmoid(gate_float)
    gate_act = gate_float * gate_sig
    gated = core_out * gate_act
    weighted_grad = norm_weight[None, :] * grad_output.astype(jnp.float32)
    norm_width = lax.axis_size("head") * gated.shape[1]
    sums = head_sum(
        jnp.stack([jnp.sum(gated * gated, axis=1), jnp.sum(weighted_grad * gated, axis=1)]),
        "head",
    )
    inv_rms = lax.rsqrt(sums[0] / norm_width + EPSILON)
    normed = gated * inv_rms[:, None]
    product = sums[1] * inv_rms
    grad_gated = inv_rms[:, None] * (weighted_grad - normed * (product / norm_width)[:, None])
    grad_core = grad_gated * gate_act
    grad_gate = grad_gated * core_out * gate_sig * (1.0 + gate_float * (1.0 - gate_sig))
    first_grads = output_back(grad_core.reshape(core_part.shape))
    first_grads = tuple(
        lax.optimization_barrier(part) if k < 4 else part for k, part in enumerate(first_grads)
    )
    exit_adjoint = chip_scan(through_all, first_grads[5], "ctx", False)
    through_grad = jnp.sum(exit_adjoint * entry_state, axis=(2, 3))
    second_grads = states_back((first_grads[4], exit_adjoint, through_grad))
    grad_input = (first_grads[0] + second_grads[0]).reshape(
        tokens_here, heads_here * HEAD_DIM
    ) + grad_core * skip_cols
    grad_step = (first_grads[1] + second_grads[1]).reshape(
        tokens_here, heads_here
    ) * jax.nn.sigmoid(shifted)
    grad_b_matrix = (first_grads[2] + second_grads[2]).reshape(tokens_here, groups_here * STATE)
    grad_c_matrix = first_grads[3].reshape(tokens_here, groups_here * STATE)
    return (
        grad_input.astype(jnp.bfloat16),
        grad_gate.astype(jnp.bfloat16),
        grad_step,
        grad_b_matrix,
        grad_c_matrix,
    )


def solution(mesh):
    return jax.shard_map(
        layer_body,
        mesh=mesh,
        in_specs=(
            P("ctx", "head"),
            P("ctx", "head"),
            P("ctx", "head"),
            P("ctx", "head"),
            P("ctx", "head"),
            P("head"),
            P("head"),
            P("head"),
            P("head"),
            P("ctx"),
            P("ctx", "head"),
        ),
        out_specs=(
            P("ctx", "head"),
            P("ctx", "head"),
            P("ctx", "head"),
            P("ctx", "head"),
            P("ctx", "head"),
        ),
        check_vma=False,
    )
```

```python
import jax
import jax.numpy as jnp
from jax import lax
from jax.sharding import PartitionSpec as P


HEAD_DIM = 64
STATE = 128
SPAN = 256


HIGHEST_PRECISION = lax.Precision.HIGHEST
MIX_PRECISION = lax.Precision.HIGH
EPSILON = 1e-05


def exclusive_scan(gain, value, move, count):
    total = jnp.zeros_like(value)
    total_gain = jnp.ones_like(gain)
    distance = 1
    while distance < count:
        gain_in, value_in = move((gain, value), distance)
        total = total + total_gain[..., None, None] * value_in
        distance *= 2
        if distance < count:
            total_gain = total_gain * gain_in
            value = value + gain[..., None, None] * value_in
            gain = gain * gain_in
    return total


def chip_scan(gain, value, axis, forward):
    size = lax.axis_size(axis)
    index = lax.axis_index(axis)
    place = index if forward else size - 1 - index
    second = place % 2
    is_second = second == 1
    half = value.shape[1] // 2

    def device(p):
        return p if forward else size - 1 - p

    def move(tree, pairs):
        return lax.ppermute(tree, axis, [(device(a), device(b)) for a, b in pairs])

    def pick(array, which):
        return lax.dynamic_slice_in_dim(array, which * half, half, axis=1)

    partners = [(p, p ^ 1) for p in range(size)]
    own_gain, own_value = pick(gain, second), pick(value, second)
    got_gain, got_value = move((pick(gain, 1 - second), pick(value, 1 - second)), partners)
    first_gain = jnp.where(is_second, got_gain, own_gain)
    first_value = jnp.where(is_second, got_value, own_value)
    second_gain = jnp.where(is_second, own_gain, got_gain)
    second_value = jnp.where(is_second, own_value, got_value)
    chip_value = second_gain[..., None, None] * first_value + second_value
    chip_gain = first_gain * second_gain

    def chip_move(tree, distance):
        step = 2 * distance
        return move(tree, [(p, p + step) for p in range(size - step)])

    prefix = exclusive_scan(chip_gain, chip_value, chip_move, size // 2)
    after_first = first_value + first_gain[..., None, None] * prefix
    own_entry = jnp.where(is_second, after_first, prefix)
    got_entry = move(jnp.where(is_second, prefix, after_first), partners)
    return jnp.where(
        is_second,
        jnp.concatenate([got_entry, own_entry], axis=1),
        jnp.concatenate([own_entry, got_entry], axis=1),
    )


def head_sum(value, axis):
    size = lax.axis_size(axis)
    spread = jnp.broadcast_to(value[None], (size,) + value.shape)
    return jnp.sum(lax.all_to_all(spread, axis, 0, 0), axis=0)


def span_mix(x_span, dt_span, b_span, c_span, log_cum, segment):
    log_rows = jnp.moveaxis(log_cum, 0, -1)
    spread = log_rows[..., :, None] - log_rows[..., None, :]
    places = jnp.arange(x_span.shape[0], dtype=jnp.int32)
    keep_mask = (
        (places[:, None] >= places[None, :]) & (segment[:, None] == segment[None, :])
    ).astype(jnp.float32)
    masked = jnp.exp(jnp.minimum(spread, 0.0)) * keep_mask
    scores = jnp.einsum("tgn,sgn->gts", c_span, b_span, precision=MIX_PRECISION)
    weights = scores[:, None] * masked * jnp.moveaxis(dt_span, 0, -1)[..., None, :]
    return jnp.einsum("ghts,sghp->tghp", weights, x_span, precision=MIX_PRECISION)


def block_decays(dt_spans, segment, decay_rate):
    length = dt_spans.shape[1]
    places = jnp.arange(length, dtype=jnp.int32)
    lower = (places[:, None] >= places[None, :]).astype(jnp.float32)
    log_cum = jnp.einsum(
        "qs,ksgh->kqgh", lower, dt_spans * decay_rate, precision=HIGHEST_PRECISION
    )
    closing = segment[:, -1]
    through = jnp.exp(log_cum[:, -1]) * (closing == 0).astype(jnp.float32)[:, None, None]
    return (log_cum, closing, through)


def local_states(x_spans, dt_spans, b_spans, segment, decay_rate):
    log_cum, closing, through = block_decays(dt_spans, segment, decay_rate)
    same_doc = (segment == closing[:, None]).astype(jnp.float32)
    tail_decay = jnp.exp(log_cum[:, -1:] - log_cum) * same_doc[:, :, None, None]
    added_terms = jnp.einsum(
        "kqgh,kqghp,kqgn->kghpn",
        tail_decay * dt_spans,
        x_spans,
        b_spans,
        precision=MIX_PRECISION,
    )

    def advance(carried_pair, item_pair):
        carry_state, product = carried_pair
        decay_now, fresh_state = item_pair
        return (
            (decay_now[..., None, None] * carry_state + fresh_state, product * decay_now),
            carry_state,
        )

    initial = (
        jnp.zeros(added_terms.shape[1:], jnp.float32),
        jnp.ones(through.shape[1:], jnp.float32),
    )
    (final_state, product), starts = lax.scan(advance, initial, (through, added_terms))
    return (starts, final_state, product)


def output_part(x_spans, dt_spans, b_spans, c_spans, segment, decay_rate, starts, entry_state):
    log_cum, _, through = block_decays(dt_spans, segment, decay_rate)

    def rolling(product, decay_now):
        return (product * decay_now, product)

    _, before = lax.scan(rolling, jnp.ones(through.shape[1:], jnp.float32), through)
    full_start = starts + before[..., None, None] * entry_state[None]
    opened = (segment == 0).astype(jnp.float32)
    entry_decay = jnp.exp(log_cum) * opened[:, :, None, None]
    carried = (
        jnp.einsum("kqgn,kghpn->kqghp", c_spans, full_start, precision=MIX_PRECISION)
        * entry_decay[..., None]
    )
    mix_block = lambda pieces: span_mix(*pieces)
    inner_part = lax.map(mix_block, (x_spans, dt_spans, b_spans, c_spans, log_cum, segment))
    inner_part = lax.optimization_barrier(inner_part)
    return inner_part + carried


def layer_body(
    ssm_input,
    gate_input,
    step_raw,
    b_matrix,
    c_matrix,
    step_bias,
    log_rate,
    skip_gain,
    norm_weight,
    doc_resets,
    grad_output,
):
    tokens_here = ssm_input.shape[0]
    heads_here = step_raw.shape[1]
    groups_here = b_matrix.shape[1] // STATE
    per_group = heads_here // groups_here
    spans = tokens_here // SPAN
    x_float = ssm_input.astype(jnp.float32)
    gate_float = gate_input.astype(jnp.float32)
    shifted = step_raw + step_bias[None, :]
    step_size = jax.nn.softplus(shifted)
    decay_rate = (-jnp.exp(log_rate)).reshape(groups_here, per_group)
    x_spans = x_float.reshape(spans, SPAN, groups_here, per_group, HEAD_DIM)
    dt_spans = step_size.reshape(spans, SPAN, groups_here, per_group)
    b_spans = b_matrix.astype(jnp.float32).reshape(spans, SPAN, groups_here, STATE)
    c_spans = c_matrix.astype(jnp.float32).reshape(spans, SPAN, groups_here, STATE)
    segment = jnp.cumsum(doc_resets.reshape(spans, SPAN), axis=1, dtype=jnp.int32)

    def states_call(x_value, dt_value, b_value):
        return local_states(x_value, dt_value, b_value, segment, decay_rate)

    (starts, end_local, through_all), states_back = jax.vjp(states_call, x_spans, dt_spans, b_spans)
    entry_state = chip_scan(through_all, end_local, "ctx", True)

    def output_call(x_value, dt_value, b_value, c_value, start_value, entry_value):
        return output_part(
            x_value, dt_value, b_value, c_value, segment, decay_rate, start_value, entry_value
        )

    core_part, output_back = jax.vjp(
        output_call, x_spans, dt_spans, b_spans, c_spans, starts, entry_state
    )
    skip_cols = jnp.repeat(skip_gain, HEAD_DIM)[None, :]
    core_out = core_part.reshape(tokens_here, heads_here * HEAD_DIM) + x_float * skip_cols
    gate_sig = jax.nn.sigmoid(gate_float)
    gate_act = gate_float * gate_sig
    gated = core_out * gate_act
    weighted_grad = norm_weight[None, :] * grad_output.astype(jnp.float32)
    norm_width = lax.axis_size("head") * gated.shape[1]
    sums = head_sum(
        jnp.stack([jnp.sum(gated * gated, axis=1), jnp.sum(weighted_grad * gated, axis=1)]),
        "head",
    )
    inv_rms = lax.rsqrt(sums[0] / norm_width + EPSILON)
    normed = gated * inv_rms[:, None]
    product = sums[1] * inv_rms
    grad_gated = inv_rms[:, None] * (weighted_grad - normed * (product / norm_width)[:, None])
    grad_core = grad_gated * gate_act
    grad_gate = grad_gated * core_out * gate_sig * (1.0 + gate_float * (1.0 - gate_sig))
    first_grads = output_back(grad_core.reshape(core_part.shape))
    first_grads = tuple(
        lax.optimization_barrier(part) if k < 4 else part for k, part in enumerate(first_grads)
    )
    exit_adjoint = chip_scan(through_all, first_grads[5], "ctx", False)
    through_grad = jnp.sum(exit_adjoint * entry_state, axis=(2, 3))
    second_grads = states_back((first_grads[4], exit_adjoint, through_grad))
    grad_input = (first_grads[0] + second_grads[0]).reshape(
        tokens_here, heads_here * HEAD_DIM
    ) + grad_core * skip_cols
    grad_step = (first_grads[1] + second_grads[1]).reshape(
        tokens_here, heads_here
    ) * jax.nn.sigmoid(shifted)
    grad_b_matrix = (first_grads[2] + second_grads[2]).reshape(tokens_here, groups_here * STATE)
    grad_c_matrix = first_grads[3].reshape(tokens_here, groups_here * STATE)
    return (
        grad_input.astype(jnp.bfloat16),
        grad_gate.astype(jnp.bfloat16),
        grad_step,
        grad_b_matrix,
        grad_c_matrix,
    )


def solution(mesh):
    return jax.shard_map(
        layer_body,
        mesh=mesh,
        in_specs=(
            P("ctx", "head"),
            P("ctx", "head"),
            P("ctx", "head"),
            P("ctx", "head"),
            P("ctx", "head"),
            P("head"),
            P("head"),
            P("head"),
            P("head"),
            P("ctx"),
            P("ctx", "head"),
        ),
        out_specs=(
            P("ctx", "head"),
            P("ctx", "head"),
            P("ctx", "head"),
            P("ctx", "head"),
            P("ctx", "head"),
        ),
        check_vma=False,
    )
```

```python
import jax
import jax.numpy as jnp
from jax import lax
from jax.sharding import PartitionSpec as P


HEAD_DIM = 64
STATE = 128
SPAN = 256


HIGHEST_PRECISION = lax.Precision.HIGHEST
MIX_PRECISION = lax.Precision.HIGH
EPSILON = 1e-05


def exclusive_scan(gain, value, move, count):
    total = jnp.zeros_like(value)
    total_gain = jnp.ones_like(gain)
    distance = 1
    while distance < count:
        gain_in, value_in = move((gain, value), distance)
        total = total + total_gain[..., None, None] * value_in
        distance *= 2
        if distance < count:
            total_gain = total_gain * gain_in
            value = value + gain[..., None, None] * value_in
            gain = gain * gain_in
    return total


def chip_scan(gain, value, axis, forward):
    size = lax.axis_size(axis)
    index = lax.axis_index(axis)
    place = index if forward else size - 1 - index
    second = place % 2
    is_second = second == 1
    half = value.shape[1] // 2

    def device(p):
        return p if forward else size - 1 - p

    def move(tree, pairs):
        return lax.ppermute(tree, axis, [(device(a), device(b)) for a, b in pairs])

    def pick(array, which):
        return lax.dynamic_slice_in_dim(array, which * half, half, axis=1)

    partners = [(p, p ^ 1) for p in range(size)]
    own_gain, own_value = pick(gain, second), pick(value, second)
    got_gain, got_value = move((pick(gain, 1 - second), pick(value, 1 - second)), partners)
    first_gain = jnp.where(is_second, got_gain, own_gain)
    first_value = jnp.where(is_second, got_value, own_value)
    second_gain = jnp.where(is_second, own_gain, got_gain)
    second_value = jnp.where(is_second, own_value, got_value)
    chip_value = second_gain[..., None, None] * first_value + second_value
    chip_gain = first_gain * second_gain

    def chip_move(tree, distance):
        step = 2 * distance
        return move(tree, [(p, p + step) for p in range(size - step)])

    prefix = exclusive_scan(chip_gain, chip_value, chip_move, size // 2)
    after_first = first_value + first_gain[..., None, None] * prefix
    own_entry = jnp.where(is_second, after_first, prefix)
    got_entry = move(jnp.where(is_second, prefix, after_first), partners)
    return jnp.where(
        is_second,
        jnp.concatenate([got_entry, own_entry], axis=1),
        jnp.concatenate([own_entry, got_entry], axis=1),
    )


def head_sum(value, axis):
    size = lax.axis_size(axis)
    spread = jnp.broadcast_to(value[None], (size,) + value.shape)
    return jnp.sum(lax.all_to_all(spread, axis, 0, 0), axis=0)


@jax.custom_vjp
def mix_apply(weights, x_span):
    return jnp.einsum("ghts,sghp->tghp", weights, x_span, precision=MIX_PRECISION)


def mix_apply_fwd(weights, x_span):
    return mix_apply(weights, x_span), (weights, x_span)


def mix_apply_bwd(saved, grad):
    weights, x_span = saved
    grad_weights = jnp.einsum("tghp,sghp->ghts", grad, x_span, precision=MIX_PRECISION)
    grad_x = jnp.einsum("ghts,tghp->sghp", weights, grad, precision=MIX_PRECISION)
    return grad_weights, grad_x


mix_apply.defvjp(mix_apply_fwd, mix_apply_bwd)


def span_mix(x_span, dt_span, b_span, c_span, log_cum, segment):
    log_rows = jnp.moveaxis(log_cum, 0, -1)
    spread = log_rows[..., :, None] - log_rows[..., None, :]
    places = jnp.arange(x_span.shape[0], dtype=jnp.int32)
    keep_mask = (
        (places[:, None] >= places[None, :]) & (segment[:, None] == segment[None, :])
    ).astype(jnp.float32)
    masked = jnp.exp(jnp.minimum(spread, 0.0)) * keep_mask
    scores = jnp.einsum("tgn,sgn->gts", c_span, b_span, precision=MIX_PRECISION)
    weights = scores[:, None] * masked * jnp.moveaxis(dt_span, 0, -1)[..., None, :]
    return mix_apply(weights, x_span)


def block_decays(dt_spans, segment, decay_rate):
    length = dt_spans.shape[1]
    places = jnp.arange(length, dtype=jnp.int32)
    lower = (places[:, None] >= places[None, :]).astype(jnp.float32)
    log_cum = jnp.einsum(
        "qs,ksgh->kqgh", lower, dt_spans * decay_rate, precision=HIGHEST_PRECISION
    )
    closing = segment[:, -1]
    through = jnp.exp(log_cum[:, -1]) * (closing == 0).astype(jnp.float32)[:, None, None]
    return (log_cum, closing, through)


def local_states(x_spans, dt_spans, b_spans, segment, decay_rate):
    log_cum, closing, through = block_decays(dt_spans, segment, decay_rate)
    same_doc = (segment == closing[:, None]).astype(jnp.float32)
    tail_decay = jnp.exp(log_cum[:, -1:] - log_cum) * same_doc[:, :, None, None]
    added_terms = jnp.einsum(
        "kqgh,kqghp,kqgn->kghpn",
        tail_decay * dt_spans,
        x_spans,
        b_spans,
        precision=MIX_PRECISION,
    )

    def advance(carried_pair, item_pair):
        carry_state, product = carried_pair
        decay_now, fresh_state = item_pair
        return (
            (decay_now[..., None, None] * carry_state + fresh_state, product * decay_now),
            carry_state,
        )

    initial = (
        jnp.zeros(added_terms.shape[1:], jnp.float32),
        jnp.ones(through.shape[1:], jnp.float32),
    )
    (final_state, product), starts = lax.scan(advance, initial, (through, added_terms))
    return (starts, final_state, product)


def output_part(x_spans, dt_spans, b_spans, c_spans, segment, decay_rate, starts, entry_state):
    log_cum, _, through = block_decays(dt_spans, segment, decay_rate)

    def rolling(product, decay_now):
        return (product * decay_now, product)

    _, before = lax.scan(rolling, jnp.ones(through.shape[1:], jnp.float32), through)
    full_start = starts + before[..., None, None] * entry_state[None]
    opened = (segment == 0).astype(jnp.float32)
    entry_decay = jnp.exp(log_cum) * opened[:, :, None, None]
    carried = (
        jnp.einsum("kqgn,kghpn->kqghp", c_spans, full_start, precision=MIX_PRECISION)
        * entry_decay[..., None]
    )
    mix_block = lambda pieces: span_mix(*pieces)
    inner_part = lax.map(mix_block, (x_spans, dt_spans, b_spans, c_spans, log_cum, segment))
    inner_part = lax.optimization_barrier(inner_part)
    return inner_part + carried


def layer_body(
    ssm_input,
    gate_input,
    step_raw,
    b_matrix,
    c_matrix,
    step_bias,
    log_rate,
    skip_gain,
    norm_weight,
    doc_resets,
    grad_output,
):
    tokens_here = ssm_input.shape[0]
    heads_here = step_raw.shape[1]
    groups_here = b_matrix.shape[1] // STATE
    per_group = heads_here // groups_here
    spans = tokens_here // SPAN
    x_float = ssm_input.astype(jnp.float32)
    gate_float = gate_input.astype(jnp.float32)
    shifted = step_raw + step_bias[None, :]
    step_size = jax.nn.softplus(shifted)
    decay_rate = (-jnp.exp(log_rate)).reshape(groups_here, per_group)
    x_spans = x_float.reshape(spans, SPAN, groups_here, per_group, HEAD_DIM)
    dt_spans = step_size.reshape(spans, SPAN, groups_here, per_group)
    b_spans = b_matrix.astype(jnp.float32).reshape(spans, SPAN, groups_here, STATE)
    c_spans = c_matrix.astype(jnp.float32).reshape(spans, SPAN, groups_here, STATE)
    segment = jnp.cumsum(doc_resets.reshape(spans, SPAN), axis=1, dtype=jnp.int32)

    def states_call(x_value, dt_value, b_value):
        return local_states(x_value, dt_value, b_value, segment, decay_rate)

    (starts, end_local, through_all), states_back = jax.vjp(states_call, x_spans, dt_spans, b_spans)
    entry_state = chip_scan(through_all, end_local, "ctx", True)

    def output_call(x_value, dt_value, b_value, c_value, start_value, entry_value):
        return output_part(
            x_value, dt_value, b_value, c_value, segment, decay_rate, start_value, entry_value
        )

    core_part, output_back = jax.vjp(
        output_call, x_spans, dt_spans, b_spans, c_spans, starts, entry_state
    )
    skip_cols = jnp.repeat(skip_gain, HEAD_DIM)[None, :]
    core_out = core_part.reshape(tokens_here, heads_here * HEAD_DIM) + x_float * skip_cols
    gate_sig = jax.nn.sigmoid(gate_float)
    gate_act = gate_float * gate_sig
    gated = core_out * gate_act
    weighted_grad = norm_weight[None, :] * grad_output.astype(jnp.float32)
    norm_width = lax.axis_size("head") * gated.shape[1]
    sums = head_sum(
        jnp.stack([jnp.sum(gated * gated, axis=1), jnp.sum(weighted_grad * gated, axis=1)]),
        "head",
    )
    inv_rms = lax.rsqrt(sums[0] / norm_width + EPSILON)
    normed = gated * inv_rms[:, None]
    product = sums[1] * inv_rms
    grad_gated = inv_rms[:, None] * (weighted_grad - normed * (product / norm_width)[:, None])
    grad_core = grad_gated * gate_act
    grad_gate = grad_gated * core_out * gate_sig * (1.0 + gate_float * (1.0 - gate_sig))
    first_grads = output_back(grad_core.reshape(core_part.shape))
    first_grads = tuple(
        lax.optimization_barrier(part) if k < 4 else part for k, part in enumerate(first_grads)
    )
    exit_adjoint = chip_scan(through_all, first_grads[5], "ctx", False)
    through_grad = jnp.sum(exit_adjoint * entry_state, axis=(2, 3))
    second_grads = states_back((first_grads[4], exit_adjoint, through_grad))
    grad_input = (first_grads[0] + second_grads[0]).reshape(
        tokens_here, heads_here * HEAD_DIM
    ) + grad_core * skip_cols
    grad_step = (first_grads[1] + second_grads[1]).reshape(
        tokens_here, heads_here
    ) * jax.nn.sigmoid(shifted)
    grad_b_matrix = (first_grads[2] + second_grads[2]).reshape(tokens_here, groups_here * STATE)
    grad_c_matrix = first_grads[3].reshape(tokens_here, groups_here * STATE)
    return (
        grad_input.astype(jnp.bfloat16),
        grad_gate.astype(jnp.bfloat16),
        grad_step,
        grad_b_matrix,
        grad_c_matrix,
    )


def solution(mesh):
    return jax.shard_map(
        layer_body,
        mesh=mesh,
        in_specs=(
            P("ctx", "head"),
            P("ctx", "head"),
            P("ctx", "head"),
            P("ctx", "head"),
            P("ctx", "head"),
            P("head"),
            P("head"),
            P("head"),
            P("head"),
            P("ctx"),
            P("ctx", "head"),
        ),
        out_specs=(
            P("ctx", "head"),
            P("ctx", "head"),
            P("ctx", "head"),
            P("ctx", "head"),
            P("ctx", "head"),
        ),
        check_vma=False,
    )
```

```python
import jax
import jax.numpy as jnp
from jax import lax
from jax.sharding import PartitionSpec as P


HEAD_DIM = 64
STATE = 128
SPAN = 256


HIGHEST_PRECISION = lax.Precision.HIGHEST
MIX_PRECISION = lax.Precision.HIGH
EPSILON = 1e-05


def exclusive_scan(gain, value, move, count):
    total = jnp.zeros_like(value)
    total_gain = jnp.ones_like(gain)
    distance = 1
    while distance < count:
        gain_in, value_in = move((gain, value), distance)
        total = total + total_gain[..., None, None] * value_in
        distance *= 2
        if distance < count:
            total_gain = total_gain * gain_in
            value = value + gain[..., None, None] * value_in
            gain = gain * gain_in
    return total


def chip_scan(gain, value, axis, forward):
    size = lax.axis_size(axis)
    index = lax.axis_index(axis)
    place = index if forward else size - 1 - index
    second = place % 2
    is_second = second == 1
    half = value.shape[1] // 2

    def device(p):
        return p if forward else size - 1 - p

    def move(tree, pairs):
        return lax.ppermute(tree, axis, [(device(a), device(b)) for a, b in pairs])

    def pick(array, which):
        return lax.dynamic_slice_in_dim(array, which * half, half, axis=1)

    partners = [(p, p ^ 1) for p in range(size)]
    own_gain, own_value = pick(gain, second), pick(value, second)
    got_gain, got_value = move((pick(gain, 1 - second), pick(value, 1 - second)), partners)
    first_gain = jnp.where(is_second, got_gain, own_gain)
    first_value = jnp.where(is_second, got_value, own_value)
    second_gain = jnp.where(is_second, own_gain, got_gain)
    second_value = jnp.where(is_second, own_value, got_value)
    chip_value = second_gain[..., None, None] * first_value + second_value
    chip_gain = first_gain * second_gain

    def chip_move(tree, distance):
        step = 2 * distance
        return move(tree, [(p, p + step) for p in range(size - step)])

    prefix = exclusive_scan(chip_gain, chip_value, chip_move, size // 2)
    after_first = first_value + first_gain[..., None, None] * prefix
    own_entry = jnp.where(is_second, after_first, prefix)
    got_entry = move(jnp.where(is_second, prefix, after_first), partners)
    return jnp.where(
        is_second,
        jnp.concatenate([got_entry, own_entry], axis=1),
        jnp.concatenate([own_entry, got_entry], axis=1),
    )


def head_sum(value, axis):
    size = lax.axis_size(axis)
    spread = jnp.broadcast_to(value[None], (size,) + value.shape)
    return jnp.sum(lax.all_to_all(spread, axis, 0, 0), axis=0)


@jax.custom_vjp
def mix_apply(weights, x_span):
    return jnp.einsum("ghts,sghp->tghp", weights, x_span, precision=MIX_PRECISION)


def mix_apply_fwd(weights, x_span):
    return mix_apply(weights, x_span), (weights, x_span)


def mix_apply_bwd(saved, grad):
    weights, x_span = saved
    grad_weights = jnp.einsum("tghp,sghp->ghts", grad, x_span, precision=MIX_PRECISION)
    grad_x = jnp.einsum("ghts,tghp->sghp", weights, grad, precision=MIX_PRECISION)
    return grad_weights, grad_x


mix_apply.defvjp(mix_apply_fwd, mix_apply_bwd)


def span_mix(x_span, dt_span, b_span, c_span, log_cum, segment):
    log_rows = jnp.moveaxis(log_cum, 0, -1)
    spread = log_rows[..., :, None] - log_rows[..., None, :]
    places = jnp.arange(x_span.shape[0], dtype=jnp.int32)
    keep_mask = (
        (places[:, None] >= places[None, :]) & (segment[:, None] == segment[None, :])
    ).astype(jnp.float32)
    masked = jnp.exp(jnp.minimum(spread, 0.0)) * keep_mask
    scores = jnp.einsum("tgn,sgn->gts", c_span, b_span, precision=MIX_PRECISION)
    weights = scores[:, None] * masked * jnp.moveaxis(dt_span, 0, -1)[..., None, :]
    return mix_apply(weights, x_span)


def block_decays(dt_spans, segment, decay_rate):
    length = dt_spans.shape[1]
    places = jnp.arange(length, dtype=jnp.int32)
    lower = (places[:, None] >= places[None, :]).astype(jnp.float32)
    log_cum = jnp.einsum(
        "qs,ksgh->kqgh", lower, dt_spans * decay_rate, precision=HIGHEST_PRECISION
    )
    closing = segment[:, -1]
    through = jnp.exp(log_cum[:, -1]) * (closing == 0).astype(jnp.float32)[:, None, None]
    return (log_cum, closing, through)


def local_states(x_spans, dt_spans, b_spans, segment, decay_rate):
    log_cum, closing, through = block_decays(dt_spans, segment, decay_rate)
    same_doc = (segment == closing[:, None]).astype(jnp.float32)
    tail_decay = jnp.exp(log_cum[:, -1:] - log_cum) * same_doc[:, :, None, None]
    added_terms = jnp.einsum(
        "kqgh,kqghp,kqgn->kghpn",
        tail_decay * dt_spans,
        x_spans,
        b_spans,
        precision=MIX_PRECISION,
    )

    def advance(carried_pair, item_pair):
        carry_state, product = carried_pair
        decay_now, fresh_state = item_pair
        return (
            (decay_now[..., None, None] * carry_state + fresh_state, product * decay_now),
            carry_state,
        )

    initial = (
        jnp.zeros(added_terms.shape[1:], jnp.float32),
        jnp.ones(through.shape[1:], jnp.float32),
    )
    (final_state, product), starts = lax.scan(advance, initial, (through, added_terms))
    return (starts, final_state, product)


def output_part(x_spans, dt_spans, b_spans, c_spans, segment, decay_rate, starts, entry_state):
    log_cum, _, through = block_decays(dt_spans, segment, decay_rate)

    def rolling(product, decay_now):
        return (product * decay_now, product)

    _, before = lax.scan(rolling, jnp.ones(through.shape[1:], jnp.float32), through)
    full_start = starts + before[..., None, None] * entry_state[None]
    opened = (segment == 0).astype(jnp.float32)
    entry_decay = jnp.exp(log_cum) * opened[:, :, None, None]
    carried = (
        jnp.einsum("kqgn,kghpn->kqghp", c_spans, full_start, precision=MIX_PRECISION)
        * entry_decay[..., None]
    )
    mix_block = lambda pieces: span_mix(*pieces)
    inner_part = lax.map(mix_block, (x_spans, dt_spans, b_spans, c_spans, log_cum, segment))
    inner_part = lax.optimization_barrier(inner_part)
    return inner_part + carried


def layer_body(
    ssm_input,
    gate_input,
    step_raw,
    b_matrix,
    c_matrix,
    step_bias,
    log_rate,
    skip_gain,
    norm_weight,
    doc_resets,
    grad_output,
):
    tokens_here = ssm_input.shape[0]
    heads_here = step_raw.shape[1]
    groups_here = b_matrix.shape[1] // STATE
    per_group = heads_here // groups_here
    spans = tokens_here // SPAN
    x_float = ssm_input.astype(jnp.float32)
    gate_float = gate_input.astype(jnp.float32)
    shifted = step_raw + step_bias[None, :]
    step_size = jax.nn.softplus(shifted)
    decay_rate = (-jnp.exp(log_rate)).reshape(groups_here, per_group)
    x_spans = x_float.reshape(spans, SPAN, groups_here, per_group, HEAD_DIM)
    dt_spans = step_size.reshape(spans, SPAN, groups_here, per_group)
    b_spans = b_matrix.astype(jnp.float32).reshape(spans, SPAN, groups_here, STATE)
    c_spans = c_matrix.astype(jnp.float32).reshape(spans, SPAN, groups_here, STATE)
    places = jnp.arange(SPAN, dtype=jnp.int32)
    lower = (places[:, None] >= places[None, :]).astype(jnp.float32)
    segment = jnp.einsum(
        "qs,ks->kq",
        lower,
        doc_resets.reshape(spans, SPAN).astype(jnp.float32),
        precision=HIGHEST_PRECISION,
    ).astype(jnp.int32)

    def states_call(x_value, dt_value, b_value):
        return local_states(x_value, dt_value, b_value, segment, decay_rate)

    (starts, end_local, through_all), states_back = jax.vjp(states_call, x_spans, dt_spans, b_spans)
    entry_state = chip_scan(through_all, end_local, "ctx", True)

    def output_call(x_value, dt_value, b_value, c_value, start_value, entry_value):
        return output_part(
            x_value, dt_value, b_value, c_value, segment, decay_rate, start_value, entry_value
        )

    core_part, output_back = jax.vjp(
        output_call, x_spans, dt_spans, b_spans, c_spans, starts, entry_state
    )
    skip_cols = jnp.repeat(skip_gain, HEAD_DIM)[None, :]
    core_out = core_part.reshape(tokens_here, heads_here * HEAD_DIM) + x_float * skip_cols
    gate_sig = jax.nn.sigmoid(gate_float)
    gate_act = gate_float * gate_sig
    gated = core_out * gate_act
    weighted_grad = norm_weight[None, :] * grad_output.astype(jnp.float32)
    norm_width = lax.axis_size("head") * gated.shape[1]
    sums = head_sum(
        jnp.stack([jnp.sum(gated * gated, axis=1), jnp.sum(weighted_grad * gated, axis=1)]),
        "head",
    )
    inv_rms = lax.rsqrt(sums[0] / norm_width + EPSILON)
    normed = gated * inv_rms[:, None]
    product = sums[1] * inv_rms
    grad_gated = inv_rms[:, None] * (weighted_grad - normed * (product / norm_width)[:, None])
    grad_core = grad_gated * gate_act
    grad_gate = grad_gated * core_out * gate_sig * (1.0 + gate_float * (1.0 - gate_sig))
    first_grads = output_back(grad_core.reshape(core_part.shape))
    first_grads = tuple(
        lax.optimization_barrier(part) if k < 4 else part for k, part in enumerate(first_grads)
    )
    exit_adjoint = chip_scan(through_all, first_grads[5], "ctx", False)
    through_grad = jnp.sum(exit_adjoint * entry_state, axis=(2, 3))
    second_grads = states_back((first_grads[4], exit_adjoint, through_grad))
    grad_input = (first_grads[0] + second_grads[0]).reshape(
        tokens_here, heads_here * HEAD_DIM
    ) + grad_core * skip_cols
    grad_step = (first_grads[1] + second_grads[1]).reshape(
        tokens_here, heads_here
    ) * jax.nn.sigmoid(shifted)
    grad_b_matrix = (first_grads[2] + second_grads[2]).reshape(tokens_here, groups_here * STATE)
    grad_c_matrix = first_grads[3].reshape(tokens_here, groups_here * STATE)
    return (
        grad_input.astype(jnp.bfloat16),
        grad_gate.astype(jnp.bfloat16),
        grad_step,
        grad_b_matrix,
        grad_c_matrix,
    )


def solution(mesh):
    return jax.shard_map(
        layer_body,
        mesh=mesh,
        in_specs=(
            P("ctx", "head"),
            P("ctx", "head"),
            P("ctx", "head"),
            P("ctx", "head"),
            P("ctx", "head"),
            P("head"),
            P("head"),
            P("head"),
            P("head"),
            P("ctx"),
            P("ctx", "head"),
        ),
        out_specs=(
            P("ctx", "head"),
            P("ctx", "head"),
            P("ctx", "head"),
            P("ctx", "head"),
            P("ctx", "head"),
        ),
        check_vma=False,
    )
```
